32 devices in a mesh: ctx: 2 (over x), req: 4 (over y, core), mp: 4 (over z).
Axes of the slice: x: 2, y: 2, z: 4, core: 2. Of those that a mesh axis runs over, the one named last changes fastest.
Arguments:
- activations: bfloat16 [4, 256, 8192], P('req', 'ctx', 'mp'), may hold values from -6 to 6
- query_base: bfloat16 [4, 256, 8192], P('req', 'ctx', 'mp'), may hold values from -9 to 9
- key_base: bfloat16 [4, 256, 1024], P('req', 'ctx', 'mp'), may hold values from -9 to 9
- plain_value_rows: bfloat16 [4, 256, 1024], P('req', 'ctx', 'mp'), may hold values from -6 to 6
- query_down: bfloat16 [8, 64, 8192], P('req', 'ctx', 'mp'), may hold values from -0.0625 to 0.0625
- query_up: bfloat16 [8, 64, 8192], P('req', 'ctx', 'mp'), may hold values from -0.75 to 0.75
- value_down: bfloat16 [8, 64, 8192], P('req', 'ctx', 'mp'), may hold values from -0.0625 to 0.0625
- value_raise_factor: bfloat16 [8, 64, 1024], P('req', 'ctx', 'mp'), may hold values from -0.75 to 0.75
- member_lists: int32 [4, 2], P('req'), may hold values from 0 to 7
- prompt_lengths: int32 [4], P('req'), may hold values from 32 to 256, as said below
Outputs:
- attended: bfloat16 [2, 4, 256, 8192], P(None, 'req', 'ctx', 'mp')
The draws below stay inside these ranges and needn't reach their ends.
Inputs may be any that keep to these rules, and one draw needn't show every extreme that they name: `prompt_lengths`: at least one prompt has all 256 positions live.
All inputs are finite; a program needn't handle non-finite values.
Results may differ from the reference program's by a relative error of at most 0.008.
Values may be sent and summed in bfloat16 or wider, within the bound.
No kernel may reach another device: no remote copies, remote signals or barrier semaphores. Data moves between devices by JAX's collectives and lax.ppermute only.
A program may use at most 64 MiB of HBM per device.

```python
import math
import jax
import jax.numpy as jnp
from jax import lax

D = 8192
QUERY_HEADS = 64
KEY_VALUE_HEADS = 8
HEAD_SIZE = 128
ADAPTER_RANK = 64
ENSEMBLE_COUNT = 8
SLOTS = 2
TOKENS_PER_SHARD = 128
PROMPT_LENGTH = 256
PROMPT_GROUPS = 4
N_CTX = 2


def drawn_rows(key):
    random_key_source = jax.random.fold_in(key, 17)
    drawn_key_rows = jnp.clip(1.5 * jax.random.normal(random_key_source, (PROMPT_GROUPS, PROMPT_LENGTH, KEY_VALUE_HEADS * HEAD_SIZE), jnp.float32), -9.0, 9.0)
    strong_rows = []
    return (drawn_key_rows, strong_rows)


def draw_key_base(key, part):
    drawn_key_rows, strong_rows = drawn_rows(key)
    return drawn_key_rows.astype(jnp.bfloat16)


def draw_query_base(key, part):
    drawn_key_rows, strong_rows = drawn_rows(key)
    query_stream = jax.random.fold_in(key, 23)
    query_matrix = jnp.clip(1.5 * jax.random.normal(query_stream, (PROMPT_GROUPS, PROMPT_LENGTH, QUERY_HEADS * HEAD_SIZE), jnp.float32), -9.0, 9.0)
    for position, strength, dominant_entries in strong_rows:
        repeated_heads = jnp.broadcast_to(dominant_entries.reshape(PROMPT_GROUPS, KEY_VALUE_HEADS, 1, HEAD_SIZE), (PROMPT_GROUPS, KEY_VALUE_HEADS, QUERY_HEADS // KEY_VALUE_HEADS, HEAD_SIZE)).reshape(PROMPT_GROUPS, QUERY_HEADS * HEAD_SIZE)
        query_matrix = query_matrix.at[:, position].set(strength * repeated_heads)
    return query_matrix.astype(jnp.bfloat16)


def draw_prompt_lengths(key, part):
    drawn = jax.random.randint(key, (PROMPT_GROUPS,), PROMPT_LENGTH // 8, PROMPT_LENGTH + 1, dtype=jnp.int32)
    longest = jax.random.randint(jax.random.fold_in(key, 5), (), 0, PROMPT_GROUPS, dtype=jnp.int32)
    return jnp.where(jnp.arange(PROMPT_GROUPS, dtype=jnp.int32) == longest, PROMPT_LENGTH, drawn).astype(jnp.int32)


def with_ends(array, own_key, least, high):
    extent = array.shape
    place = [jax.random.randint(jax.random.fold_in(own_key, axis), (), 0, extent[axis]) for axis in range(len(extent))]
    array = array.at[tuple(place)].set(least)
    longest = extent.index(max(extent))
    place[longest] = (place[longest] + 1) % extent[longest]
    return array.at[tuple(place)].set(high)


def block_levels(own_key, shape, shards, low, high):
    gain = 1.0
    for dim, blocks in shards:
        draws = jax.random.uniform(jax.random.fold_in(jax.random.fold_in(own_key, 6), dim), (blocks,), jnp.float32, low / len(shards), high / len(shards))
        gain = gain * jnp.repeat(jnp.exp(draws), shape[dim] // blocks).reshape((-1,) + (1,) * (len(shape) - 1 - dim))
    return gain


def bell_draw(own_key, dims, scale, most, shards=(), kind=jnp.bfloat16):
    array = jax.random.normal(own_key, dims, jnp.float32) * scale
    if len(shards) > 0:
        array = block_levels(own_key, dims, shards, -0.22, 0.18) * array
    return jnp.clip(array, min=-most, max=most).astype(kind)


def setup_inputs(seed: int = 0) -> dict:
    seeds = jax.random.split(jax.random.key(seed), 11)
    activations = bell_draw(seeds[0], (PROMPT_GROUPS, PROMPT_LENGTH, D), 1.0, 6.0, ((0, 4), (1, 2), (2, 4)))
    query_base = draw_query_base(jax.random.fold_in(seeds[10], 71), 0)
    key_base = draw_key_base(jax.random.fold_in(seeds[10], 71), 0)
    plain_value_rows = bell_draw(seeds[3], (PROMPT_GROUPS, PROMPT_LENGTH, KEY_VALUE_HEADS * HEAD_SIZE), 1.0, 6.0, ((0, 4), (1, 2), (2, 4)))
    query_down = bell_draw(seeds[4], (ENSEMBLE_COUNT, ADAPTER_RANK, D), D ** -0.5, 0.0625, ((0, 4), (1, 2), (2, 4)))
    query_up = bell_draw(seeds[5], (ENSEMBLE_COUNT, ADAPTER_RANK, QUERY_HEADS * HEAD_SIZE), ADAPTER_RANK ** -0.5, 0.75, ((0, 4), (1, 2), (2, 4)))
    value_down = bell_draw(seeds[6], (ENSEMBLE_COUNT, ADAPTER_RANK, D), D ** -0.5, 0.0625, ((0, 4), (1, 2), (2, 4)))
    value_raise_factor = bell_draw(seeds[7], (ENSEMBLE_COUNT, ADAPTER_RANK, KEY_VALUE_HEADS * HEAD_SIZE), ADAPTER_RANK ** -0.5, 0.75, ((0, 4), (1, 2), (2, 4)))
    member_lists = with_ends(jax.random.randint(seeds[8], (PROMPT_GROUPS, SLOTS), 0, ENSEMBLE_COUNT), jax.random.fold_in(seeds[8], 1), 0, ENSEMBLE_COUNT - 1).astype(jnp.int32)
    prompt_lengths = draw_prompt_lengths(jax.random.fold_in(seeds[10], 71), 0)
    return {"activations": activations, "query_base": query_base, "key_base": key_base, "plain_value_rows": plain_value_rows, "query_down": query_down, "query_up": query_up, "value_down": value_down, "value_raise_factor": value_raise_factor, "member_lists": member_lists, "prompt_lengths": prompt_lengths}


def attend_block(block_index, query_matrix, rows_of_keys, value_matrix, live_length):
    starting_row = block_index * TOKENS_PER_SHARD
    group_portion = QUERY_HEADS // KEY_VALUE_HEADS
    rows_of_queries = lax.dynamic_slice_in_dim(query_matrix, starting_row, TOKENS_PER_SHARD, 0).reshape(TOKENS_PER_SHARD, KEY_VALUE_HEADS, group_portion, HEAD_SIZE).astype(jnp.float32)
    heads_of_keys = rows_of_keys.reshape(PROMPT_LENGTH, KEY_VALUE_HEADS, HEAD_SIZE).astype(jnp.float32)
    heads_of_values = value_matrix.reshape(PROMPT_LENGTH, KEY_VALUE_HEADS, HEAD_SIZE).astype(jnp.float32)
    inverse = 1.0 / math.sqrt(HEAD_SIZE)
    scores = jnp.einsum('rgjd,kgd->gjrk', rows_of_queries, heads_of_keys) * inverse
    positions = starting_row + jnp.arange(TOKENS_PER_SHARD, dtype=jnp.int32)
    key_positions = jnp.arange(PROMPT_LENGTH, dtype=jnp.int32)
    visible = (key_positions[None, :] <= positions[:, None]) & (key_positions[None, :] < live_length)
    masked = jnp.where(visible, scores, -1e+30)
    row_max = lax.optimization_barrier(jnp.max(masked, axis=-1))
    raised = jnp.where(visible, jnp.exp(masked - row_max[..., None]), 0.0)
    totals = lax.optimization_barrier(jnp.sum(raised, axis=-1))
    weights = lax.optimization_barrier(raised.astype(jnp.bfloat16)).astype(jnp.float32)
    blended = jnp.einsum('gjrk,kgd->rgjd', weights, heads_of_values)
    blended = blended / jnp.transpose(totals, (2, 0, 1))[..., None]
    return blended.reshape(TOKENS_PER_SHARD, QUERY_HEADS * HEAD_SIZE).astype(jnp.bfloat16)

def reference(activations, query_base, key_base, plain_value_rows, query_down, query_up, value_down, value_raise_factor, member_lists, prompt_lengths):
    outputs = []
    for slot_index in range(SLOTS):
        per_group = []
        for group_index in range(PROMPT_GROUPS):
            member_id = member_lists[group_index, slot_index]
            down_query = lax.dynamic_index_in_dim(query_down, member_id, 0, keepdims=False)
            up_query = lax.dynamic_index_in_dim(query_up, member_id, 0, keepdims=False)
            down_value = lax.dynamic_index_in_dim(value_down, member_id, 0, keepdims=False)
            up_value = lax.dynamic_index_in_dim(value_raise_factor, member_id, 0, keepdims=False)
            tokens = activations[group_index]
            rank_query = jnp.dot(tokens, down_query.T, preferred_element_type=jnp.float32).astype(jnp.bfloat16)
            rank_value = jnp.dot(tokens, down_value.T, preferred_element_type=jnp.float32).astype(jnp.bfloat16)
            query_matrix = (query_base[group_index].astype(jnp.float32) + jnp.dot(rank_query, up_query, preferred_element_type=jnp.float32)).astype(jnp.bfloat16)
            value_matrix = (plain_value_rows[group_index].astype(jnp.float32) + jnp.dot(rank_value, up_value, preferred_element_type=jnp.float32)).astype(jnp.bfloat16)
            rows_of_keys = key_base[group_index]
            live_length = prompt_lengths[group_index]
            blocks = lax.map(lambda block_index: attend_block(block_index, query_matrix, rows_of_keys, value_matrix, live_length), jnp.arange(N_CTX, dtype=jnp.int32))
            per_group.append(blocks.reshape(PROMPT_LENGTH, QUERY_HEADS * HEAD_SIZE))
        outputs.append(jnp.stack(per_group))
    return jnp.stack(outputs)
```

```python
import math

import jax
import jax.numpy as jnp
from jax import lax
from jax.sharding import PartitionSpec as P

HEAD_SIZE = 128


def block_rows(total_rows):
    if total_rows <= 512:
        return total_rows
    for candidate in range(512, 0, -1):
        if total_rows % candidate == 0:
            return candidate
    return total_rows


def swap(value, axis, bit):
    size = lax.axis_size(axis)
    return lax.ppermute(value, axis, [(i, i ^ bit) for i in range(size)])


def ctx_gather(mine, dim, ordered):
    if lax.axis_size("ctx") == 2:
        other = swap(mine, "ctx", 1)
        if not ordered:
            return jnp.concatenate([mine, other], axis=dim)
        first = lax.axis_index("ctx") == 0
        low = jnp.where(first, mine, other)
        high = jnp.where(first, other, mine)
        return jnp.concatenate([low, high], axis=dim)
    return lax.all_gather(mine, "ctx", axis=dim, tiled=True)


def mp_sum(values):
    size = lax.axis_size("mp")
    if size & (size - 1):
        return lax.psum(values, "mp")
    bit = 1
    while bit < size:
        values = jax.tree.map(lambda a, b: a + b, values, swap(values, "mp", bit))
        bit *= 2
    return values


def select_members(factor_set, member_ids, member_lists):
    local_count = factor_set[0].shape[0]
    req_size = lax.axis_size("req")
    if req_size != 4:
        everything = [lax.all_gather(f, "req", axis=0, tiled=True) for f in factor_set]
        return [
            jnp.stack([lax.dynamic_index_in_dim(f, m, 0, keepdims=False) for m in member_ids])
            for f in everything
        ]
    req = lax.axis_index("req")
    core = req % 2
    row = req // 2
    row_span = 2 * local_count
    partners = swap(tuple(factor_set), "req", 1)
    far_ids = swap(member_lists, "req", 2)[0]

    def pick(own, partner, index):
        mine = lax.dynamic_index_in_dim(own, index % local_count, 0, keepdims=False)
        theirs = lax.dynamic_index_in_dim(partner, index % local_count, 0, keepdims=False)
        return jnp.where(index // local_count == core, mine, theirs)

    outgoing = tuple(
        jnp.stack([pick(own, partner, far_ids[s] % row_span) for s in range(far_ids.shape[0])])
        for own, partner in zip(factor_set, partners)
    )
    incoming = swap(outgoing, "req", 2)
    chosen = []
    for own, partner, received in zip(factor_set, partners, incoming):
        slots = []
        for s in range(member_ids.shape[0]):
            m = member_ids[s]
            near = pick(own, partner, m % row_span)
            slots.append(jnp.where(m // row_span == row, near, received[s]))
        chosen.append(jnp.stack(slots))
    return chosen


def per_device(
    activations,
    query_base,
    key_base,
    plain_value_rows,
    query_down,
    query_up,
    value_down,
    value_raise_factor,
    member_lists,
    prompt_lengths,
):
    row_count = activations.shape[1]
    member_ids = member_lists[0]
    halves = select_members(
        (query_down, value_down, query_up, value_raise_factor), member_ids, member_lists
    )
    down_query, down_value, up_query, up_value = [ctx_gather(h, 1, False) for h in halves]
    tokens = activations[0]
    rank_query = jnp.einsum("rd,skd->rsk", tokens, down_query, preferred_element_type=jnp.float32)
    rank_value = jnp.einsum("rd,skd->rsk", tokens, down_value, preferred_element_type=jnp.float32)
    rank_query, rank_value = mp_sum((rank_query, rank_value))
    rank_query = rank_query.astype(jnp.bfloat16)
    rank_value = rank_value.astype(jnp.bfloat16)
    query_matrix = (
        query_base[0][:, None, :]
        + jnp.einsum("rsk,skc->rsc", rank_query, up_query, preferred_element_type=jnp.float32)
    ).astype(jnp.bfloat16)
    slot_count = query_matrix.shape[1]
    group_count = key_base.shape[2] // HEAD_SIZE
    group_portion = query_matrix.shape[2] // (group_count * HEAD_SIZE)
    grouped = query_matrix.reshape(row_count, slot_count, group_count, group_portion, HEAD_SIZE)
    rows_of_keys = key_base[0]
    positions = lax.axis_index("ctx") * row_count + jnp.arange(row_count, dtype=jnp.int32)
    live_length = prompt_lengths[0]
    inverse = 1.0 / math.sqrt(HEAD_SIZE)

    def update(running, key_block, value_block, key_start):
        run_max, run_total, accumulated = running
        block_length = key_block.shape[0]
        heads_of_keys = key_block.reshape(block_length, group_count, HEAD_SIZE)
        heads_of_values = value_block.reshape(block_length, slot_count, group_count, HEAD_SIZE)
        scores = (
            jnp.einsum(
                "rsgjd,kgd->sgjrk", grouped, heads_of_keys, preferred_element_type=jnp.float32
            )
            * inverse
        )
        key_positions = key_start + jnp.arange(block_length, dtype=jnp.int32)
        visible = (key_positions[None, :] <= positions[:, None]) & (
            key_positions[None, :] < live_length
        )
        masked = jnp.where(visible, scores, -1e30)
        new_max = jnp.maximum(run_max, jnp.max(masked, axis=-1))
        weights = jnp.where(visible, jnp.exp(masked - new_max[..., None]), 0.0)
        factor = jnp.exp(run_max - new_max)
        new_total = run_total * factor + jnp.sum(weights, axis=-1)
        new_accumulated = accumulated * factor[..., None] + jnp.einsum(
            "sgjrk,ksgd->sgjrd",
            weights.astype(jnp.bfloat16),
            heads_of_values,
            preferred_element_type=jnp.float32,
        )
        return (new_max, new_total, new_accumulated)

    initial = (
        jnp.full((slot_count, group_count, group_portion, row_count), -1e30, jnp.float32),
        jnp.zeros((slot_count, group_count, group_portion, row_count), jnp.float32),
        jnp.zeros((slot_count, group_count, group_portion, row_count, HEAD_SIZE), jnp.float32),
    )
    base_rows = plain_value_rows[0]
    built = (
        base_rows[:, None, :]
        + jnp.einsum("rsk,skc->rsc", rank_value, up_value, preferred_element_type=jnp.float32)
    ).astype(jnp.bfloat16)
    packed = built.reshape(row_count, slot_count * group_count * HEAD_SIZE)
    key_piece = ctx_gather(rows_of_keys, 0, True)
    value_piece = ctx_gather(packed, 0, True)
    piece_rows = key_piece.shape[0]
    step_rows = block_rows(piece_rows)

    def advance(block_index, current):
        offset = block_index * step_rows
        key_block = lax.dynamic_slice_in_dim(key_piece, offset, step_rows, 0)
        value_block = lax.dynamic_slice_in_dim(value_piece, offset, step_rows, 0)
        return update(current, key_block, value_block, offset)

    run_max, run_total, accumulated = lax.fori_loop(0, piece_rows // step_rows, advance, initial)
    result = accumulated / run_total[..., None]
    result = (
        jnp.transpose(result, (0, 3, 1, 2, 4))
        .reshape(slot_count, row_count, group_count * group_portion * HEAD_SIZE)
        .astype(jnp.bfloat16)
    )
    return result[:, None]


def solution(mesh):
    in_specs = (
        P("req", "ctx", "mp"),
        P("req", "ctx", "mp"),
        P("req", "ctx", "mp"),
        P("req", "ctx", "mp"),
        P("req", "ctx", "mp"),
        P("req", "ctx", "mp"),
        P("req", "ctx", "mp"),
        P("req", "ctx", "mp"),
        P("req", None),
        P("req"),
    )
    out_specs = P(None, "req", "ctx", "mp")
    return jax.shard_map(
        per_device, mesh=mesh, in_specs=in_specs, out_specs=out_specs, check_vma=False
    )
```

```python
import math

import jax
import jax.numpy as jnp
from jax import lax
from jax.sharding import PartitionSpec as P

HEAD_SIZE = 128


def block_rows(total_rows):
    if total_rows <= 512:
        return total_rows
    for candidate in range(512, 0, -1):
        if total_rows % candidate == 0:
            return candidate
    return total_rows


def swap(value, axis, bit):
    size = lax.axis_size(axis)
    return lax.ppermute(value, axis, [(i, i ^ bit) for i in range(size)])


def ctx_gather(mine, dim, ordered):
    if lax.axis_size("ctx") == 2:
        other = swap(mine, "ctx", 1)
        if not ordered:
            return jnp.concatenate([mine, other], axis=dim)
        first = lax.axis_index("ctx") == 0
        low = jnp.where(first, mine, other)
        high = jnp.where(first, other, mine)
        return jnp.concatenate([low, high], axis=dim)
    return lax.all_gather(mine, "ctx", axis=dim, tiled=True)


def mp_sum(value):
    size = lax.axis_size("mp")
    if size & (size - 1):
        return lax.psum(value, "mp")
    total = value
    for bit in range(1, size):
        total = total + swap(value, "mp", bit)
    return total


def select_members(factor_set, member_ids, member_lists):
    local_count = factor_set[0].shape[0]
    req_size = lax.axis_size("req")
    if req_size != 4:
        everything = [lax.all_gather(f, "req", axis=0, tiled=True) for f in factor_set]
        return [
            jnp.stack([lax.dynamic_index_in_dim(f, m, 0, keepdims=False) for m in member_ids])
            for f in everything
        ]
    req = lax.axis_index("req")
    core = req % 2
    row = req // 2
    row_span = 2 * local_count
    partners = swap(tuple(factor_set), "req", 1)
    far_ids = swap(member_lists, "req", 2)[0]

    def pick(own, partner, index):
        mine = lax.dynamic_index_in_dim(own, index % local_count, 0, keepdims=False)
        theirs = lax.dynamic_index_in_dim(partner, index % local_count, 0, keepdims=False)
        return jnp.where(index // local_count == core, mine, theirs)

    outgoing = tuple(
        jnp.stack([pick(own, partner, far_ids[s] % row_span) for s in range(far_ids.shape[0])])
        for own, partner in zip(factor_set, partners)
    )
    incoming = swap(outgoing, "req", 2)
    chosen = []
    for own, partner, received in zip(factor_set, partners, incoming):
        slots = []
        for s in range(member_ids.shape[0]):
            m = member_ids[s]
            near = pick(own, partner, m % row_span)
            slots.append(jnp.where(m // row_span == row, near, received[s]))
        chosen.append(jnp.stack(slots))
    return chosen


def per_device(
    activations,
    query_base,
    key_base,
    plain_value_rows,
    query_down,
    query_up,
    value_down,
    value_raise_factor,
    member_lists,
    prompt_lengths,
):
    row_count = activations.shape[1]
    member_ids = member_lists[0]
    local_count, rank_part, width = query_down.shape
    up_width = query_up.shape[2]
    downs = jnp.stack([query_down, value_down], axis=1)
    ups = jnp.concatenate([query_up, value_raise_factor], axis=2)
    down_half, up_half = select_members((downs, ups), member_ids, member_lists)
    downs = ctx_gather(down_half, 2, False)
    ups = ctx_gather(up_half, 1, False)
    tokens = activations[0]
    ranks = jnp.einsum("rd,sfkd->rfsk", tokens, downs, preferred_element_type=jnp.float32)
    ranks = mp_sum(ranks).astype(jnp.bfloat16)
    rank_query = ranks[:, 0]
    rank_value = ranks[:, 1]
    up_query = ups[..., :up_width]
    up_value = ups[..., up_width:]
    query_matrix = (
        query_base[0][:, None, :]
        + jnp.einsum("rsk,skc->rsc", rank_query, up_query, preferred_element_type=jnp.float32)
    ).astype(jnp.bfloat16)
    slot_count = query_matrix.shape[1]
    group_count = key_base.shape[2] // HEAD_SIZE
    group_portion = query_matrix.shape[2] // (group_count * HEAD_SIZE)
    grouped = query_matrix.reshape(row_count, slot_count, group_count, group_portion, HEAD_SIZE)
    rows_of_keys = key_base[0]
    positions = lax.axis_index("ctx") * row_count + jnp.arange(row_count, dtype=jnp.int32)
    live_length = prompt_lengths[0]
    inverse = 1.0 / math.sqrt(HEAD_SIZE)

    def update(running, key_block, value_block, key_start):
        run_max, run_total, accumulated = running
        block_length = key_block.shape[0]
        heads_of_keys = key_block.reshape(block_length, group_count, HEAD_SIZE)
        heads_of_values = value_block.reshape(block_length, slot_count, group_count, HEAD_SIZE)
        scores = (
            jnp.einsum(
                "rsgjd,kgd->sgjrk", grouped, heads_of_keys, preferred_element_type=jnp.float32
            )
            * inverse
        )
        key_positions = key_start + jnp.arange(block_length, dtype=jnp.int32)
        visible = (key_positions[None, :] <= positions[:, None]) & (
            key_positions[None, :] < live_length
        )
        masked = jnp.where(visible, scores, -1e30)
        new_max = jnp.maximum(run_max, jnp.max(masked, axis=-1))
        weights = jnp.where(visible, jnp.exp(masked - new_max[..., None]), 0.0)
        factor = jnp.exp(run_max - new_max)
        new_total = run_total * factor + jnp.sum(weights, axis=-1)
        new_accumulated = accumulated * factor[..., None] + jnp.einsum(
            "sgjrk,ksgd->sgjrd",
            weights.astype(jnp.bfloat16),
            heads_of_values,
            preferred_element_type=jnp.float32,
        )
        return (new_max, new_total, new_accumulated)

    initial = (
        jnp.full((slot_count, group_count, group_portion, row_count), -1e30, jnp.float32),
        jnp.zeros((slot_count, group_count, group_portion, row_count), jnp.float32),
        jnp.zeros((slot_count, group_count, group_portion, row_count, HEAD_SIZE), jnp.float32),
    )
    base_rows = plain_value_rows[0]
    built = (
        base_rows[:, None, :]
        + jnp.einsum("rsk,skc->rsc", rank_value, up_value, preferred_element_type=jnp.float32)
    ).astype(jnp.bfloat16)
    packed = built.reshape(row_count, slot_count * group_count * HEAD_SIZE)
    key_piece = ctx_gather(rows_of_keys, 0, True)
    value_piece = ctx_gather(packed, 0, True)
    piece_rows = key_piece.shape[0]
    step_rows = block_rows(piece_rows)

    def advance(block_index, current):
        offset = block_index * step_rows
        key_block = lax.dynamic_slice_in_dim(key_piece, offset, step_rows, 0)
        value_block = lax.dynamic_slice_in_dim(value_piece, offset, step_rows, 0)
        return update(current, key_block, value_block, offset)

    run_max, run_total, accumulated = lax.fori_loop(0, piece_rows // step_rows, advance, initial)
    result = accumulated / run_total[..., None]
    result = (
        jnp.transpose(result, (0, 3, 1, 2, 4))
        .reshape(slot_count, row_count, group_count * group_portion * HEAD_SIZE)
        .astype(jnp.bfloat16)
    )
    return result[:, None]


def solution(mesh):
    in_specs = (
        P("req", "ctx", "mp"),
        P("req", "ctx", "mp"),
        P("req", "ctx", "mp"),
        P("req", "ctx", "mp"),
        P("req", "ctx", "mp"),
        P("req", "ctx", "mp"),
        P("req", "ctx", "mp"),
        P("req", "ctx", "mp"),
        P("req", None),
        P("req"),
    )
    out_specs = P(None, "req", "ctx", "mp")
    return jax.shard_map(
        per_device, mesh=mesh, in_specs=in_specs, out_specs=out_specs, check_vma=False
    )
```

```python
import math

import jax
import jax.numpy as jnp
from jax import lax
from jax.sharding import PartitionSpec as P

HEAD_SIZE = 128


def block_rows(total_rows):
    if total_rows <= 512:
        return total_rows
    for candidate in range(512, 0, -1):
        if total_rows % candidate == 0:
            return candidate
    return total_rows


def swap(value, axis, bit):
    size = lax.axis_size(axis)
    return lax.ppermute(value, axis, [(i, i ^ bit) for i in range(size)])


def ctx_gather(mine, dim, ordered):
    if lax.axis_size("ctx") == 2:
        other = swap(mine, "ctx", 1)
        if not ordered:
            return jnp.concatenate([mine, other], axis=dim)
        first = lax.axis_index("ctx") == 0
        low = jnp.where(first, mine, other)
        high = jnp.where(first, other, mine)
        return jnp.concatenate([low, high], axis=dim)
    return lax.all_gather(mine, "ctx", axis=dim, tiled=True)


def mp_sum(value):
    size = lax.axis_size("mp")
    if size & (size - 1):
        return lax.psum(value, "mp")
    total = value
    for bit in range(1, size):
        total = total + swap(value, "mp", bit)
    return total


def select_members(factor_set, member_ids, member_lists):
    local_count = factor_set[0].shape[0]
    req_size = lax.axis_size("req")
    if req_size != 4:
        everything = [lax.all_gather(f, "req", axis=0, tiled=True) for f in factor_set]
        return [
            jnp.stack([lax.dynamic_index_in_dim(f, m, 0, keepdims=False) for m in member_ids])
            for f in everything
        ]
    req = lax.axis_index("req")
    core = req % 2
    row = req // 2
    row_span = 2 * local_count
    partners = swap(tuple(factor_set), "req", 1)
    far_ids = swap(member_lists, "req", 2)[0]

    def pick(own, partner, index):
        mine = lax.dynamic_index_in_dim(own, index % local_count, 0, keepdims=False)
        theirs = lax.dynamic_index_in_dim(partner, index % local_count, 0, keepdims=False)
        return jnp.where(index // local_count == core, mine, theirs)

    outgoing = tuple(
        jnp.stack([pick(own, partner, far_ids[s] % row_span) for s in range(far_ids.shape[0])])
        for own, partner in zip(factor_set, partners)
    )
    incoming = swap(outgoing, "req", 2)
    chosen = []
    for own, partner, received in zip(factor_set, partners, incoming):
        slots = []
        for s in range(member_ids.shape[0]):
            m = member_ids[s]
            near = pick(own, partner, m % row_span)
            slots.append(jnp.where(m // row_span == row, near, received[s]))
        chosen.append(jnp.stack(slots))
    return chosen


def attend(grouped, keys, values, key_positions, positions, live_length, slot_count):
    row_count, _, group_count, group_portion, _ = grouped.shape
    inverse = 1.0 / math.sqrt(HEAD_SIZE)

    def update(running, key_block, value_block, block_positions):
        run_max, run_total, accumulated = running
        block_length = key_block.shape[0]
        heads_of_keys = key_block.reshape(block_length, group_count, HEAD_SIZE)
        heads_of_values = value_block.reshape(block_length, slot_count, group_count, HEAD_SIZE)
        scores = (
            jnp.einsum(
                "rsgjd,kgd->sgjrk", grouped, heads_of_keys, preferred_element_type=jnp.float32
            )
            * inverse
        )
        visible = (block_positions[None, :] <= positions[:, None]) & (
            block_positions[None, :] < live_length
        )
        masked = jnp.where(visible, scores, -1e30)
        new_max = jnp.maximum(run_max, jnp.max(masked, axis=-1))
        weights = jnp.where(visible, jnp.exp(masked - new_max[..., None]), 0.0)
        factor = jnp.exp(run_max - new_max)
        new_total = run_total * factor + jnp.sum(weights, axis=-1)
        new_accumulated = accumulated * factor[..., None] + jnp.einsum(
            "sgjrk,ksgd->sgjrd",
            weights.astype(jnp.bfloat16),
            heads_of_values,
            preferred_element_type=jnp.float32,
        )
        return (new_max, new_total, new_accumulated)

    initial = (
        jnp.full((slot_count, group_count, group_portion, row_count), -1e30, jnp.float32),
        jnp.zeros((slot_count, group_count, group_portion, row_count), jnp.float32),
        jnp.zeros((slot_count, group_count, group_portion, row_count, HEAD_SIZE), jnp.float32),
    )
    piece_rows = keys.shape[0]
    step_rows = block_rows(piece_rows)

    def advance(block_index, current):
        offset = block_index * step_rows
        key_block = lax.dynamic_slice_in_dim(keys, offset, step_rows, 0)
        value_block = lax.dynamic_slice_in_dim(values, offset, step_rows, 0)
        block_positions = lax.dynamic_slice_in_dim(key_positions, offset, step_rows, 0)
        return update(current, key_block, value_block, block_positions)

    run_max, run_total, accumulated = lax.fori_loop(0, piece_rows // step_rows, advance, initial)
    result = accumulated / run_total[..., None]
    return (
        jnp.transpose(result, (0, 3, 1, 2, 4))
        .reshape(slot_count, row_count, group_count * group_portion * HEAD_SIZE)
        .astype(jnp.bfloat16)
    )


def per_device(
    activations,
    query_base,
    key_base,
    plain_value_rows,
    query_down,
    query_up,
    value_down,
    value_raise_factor,
    member_lists,
    prompt_lengths,
):
    row_count = activations.shape[1]
    member_ids = member_lists[0]
    slot_count = member_ids.shape[0]
    up_width = query_up.shape[2]
    group_count = key_base.shape[2] // HEAD_SIZE
    ctx = lax.axis_index("ctx")
    positions = ctx * row_count + jnp.arange(row_count, dtype=jnp.int32)
    downs = jnp.stack([query_down, value_down], axis=1)
    ups = jnp.concatenate([query_up, value_raise_factor], axis=2)
    down_half, up_half = select_members((downs, ups), member_ids, member_lists)
    ups = ctx_gather(up_half, 1, False)
    up_query = ups[..., :up_width]
    up_value = ups[..., up_width:]
    if lax.axis_size("ctx") == 2:
        tokens = ctx_gather(activations[0], 0, False)
        partial = jnp.einsum("rd,sfkd->rfsk", tokens, down_half, preferred_element_type=jnp.float32)
        mine = mp_sum(partial).astype(jnp.bfloat16)
        theirs = swap(mine, "ctx", 1)
        theirs = jnp.concatenate([theirs[row_count:], theirs[:row_count]], axis=0)
        ranks = jnp.concatenate([mine, theirs], axis=3)
        value_rows = ctx_gather(plain_value_rows[0], 0, False)
        keys = ctx_gather(key_base[0], 0, False)
        own_keys = jnp.arange(row_count, dtype=jnp.int32)
        key_positions = jnp.concatenate(
            [ctx * row_count + own_keys, (1 - ctx) * row_count + own_keys]
        )
        rank_query = ranks[:row_count, 0]
        rank_value = ranks[:, 1]
    else:
        downs = ctx_gather(down_half, 2, False)
        partial = jnp.einsum(
            "rd,sfkd->rfsk", activations[0], downs, preferred_element_type=jnp.float32
        )
        ranks = mp_sum(partial).astype(jnp.bfloat16)
        rank_query = ranks[:, 0]
        rank_value = ranks[:, 1]
        value_rows = plain_value_rows[0]
        keys = ctx_gather(key_base[0], 0, True)
        key_positions = jnp.arange(keys.shape[0], dtype=jnp.int32)
    query_matrix = (
        query_base[0][:, None, :]
        + jnp.einsum("rsk,skc->rsc", rank_query, up_query, preferred_element_type=jnp.float32)
    ).astype(jnp.bfloat16)
    group_portion = query_matrix.shape[2] // (group_count * HEAD_SIZE)
    grouped = query_matrix.reshape(row_count, slot_count, group_count, group_portion, HEAD_SIZE)
    built = (
        value_rows[:, None, :]
        + jnp.einsum("rsk,skc->rsc", rank_value, up_value, preferred_element_type=jnp.float32)
    ).astype(jnp.bfloat16)
    values = built.reshape(built.shape[0], slot_count * group_count * HEAD_SIZE)
    if lax.axis_size("ctx") != 2:
        values = ctx_gather(values, 0, True)
    result = attend(
        grouped, keys, values, key_positions, positions, prompt_lengths[0], slot_count
    )
    return result[:, None]


def solution(mesh):
    in_specs = (
        P("req", "ctx", "mp"),
        P("req", "ctx", "mp"),
        P("req", "ctx", "mp"),
        P("req", "ctx", "mp"),
        P("req", "ctx", "mp"),
        P("req", "ctx", "mp"),
        P("req", "ctx", "mp"),
        P("req", "ctx", "mp"),
        P("req", None),
        P("req"),
    )
    out_specs = P(None, "req", "ctx", "mp")
    return jax.shard_map(
        per_device, mesh=mesh, in_specs=in_specs, out_specs=out_specs, check_vma=False
    )
```

```python
import math

import jax
import jax.numpy as jnp
from jax import lax
from jax.sharding import PartitionSpec as P

HEAD_SIZE = 128


def block_rows(total_rows):
    if total_rows <= 512:
        return total_rows
    for candidate in range(512, 0, -1):
        if total_rows % candidate == 0:
            return candidate
    return total_rows


def swap(value, axis, bit):
    size = lax.axis_size(axis)
    return lax.ppermute(value, axis, [(i, i ^ bit) for i in range(size)])


def ctx_gather(mine, dim, ordered):
    if lax.axis_size("ctx") == 2:
        other = swap(mine, "ctx", 1)
        if not ordered:
            return jnp.concatenate([mine, other], axis=dim)
        first = lax.axis_index("ctx") == 0
        low = jnp.where(first, mine, other)
        high = jnp.where(first, other, mine)
        return jnp.concatenate([low, high], axis=dim)
    return lax.all_gather(mine, "ctx", axis=dim, tiled=True)


def mp_sum(value):
    size = lax.axis_size("mp")
    if size & (size - 1):
        return lax.psum(value, "mp")
    total = value
    for bit in range(1, size):
        total = total + swap(value, "mp", bit)
    return total


def select_members(factor_set, member_ids, member_lists):
    local_count = factor_set[0].shape[0]
    req_size = lax.axis_size("req")
    if req_size != 4:
        everything = [lax.all_gather(f, "req", axis=0, tiled=True) for f in factor_set]
        return [
            jnp.stack([lax.dynamic_index_in_dim(f, m, 0, keepdims=False) for m in member_ids])
            for f in everything
        ]
    req = lax.axis_index("req")
    core = req % 2
    row = req // 2
    row_span = 2 * local_count
    far_ids = swap(member_lists, "req", 2)[0]

    def pick(own, partner, index):
        mine = lax.dynamic_index_in_dim(own, index % local_count, 0, keepdims=False)
        theirs = lax.dynamic_index_in_dim(partner, index % local_count, 0, keepdims=False)
        return jnp.where(index // local_count == core, mine, theirs)

    partners = []
    incoming = []
    previous = None
    for own in factor_set:
        if previous is not None:
            own = lax.optimization_barrier((own, previous[0]))[0]
        partner = swap(own, "req", 1)
        outgoing = jnp.stack(
            [pick(own, partner, far_ids[s] % row_span) for s in range(far_ids.shape[0])]
        )
        if previous is not None:
            outgoing = lax.optimization_barrier((outgoing, previous[1]))[0]
        received = swap(outgoing, "req", 2)
        partners.append(partner)
        incoming.append(received)
        previous = (partner, received)
    chosen = []
    for own, partner, received in zip(factor_set, partners, incoming):
        slots = []
        for s in range(member_ids.shape[0]):
            m = member_ids[s]
            near = pick(own, partner, m % row_span)
            slots.append(jnp.where(m // row_span == row, near, received[s]))
        chosen.append(jnp.stack(slots))
    return chosen


def attend(grouped, keys, values, key_positions, positions, live_length, slot_count):
    row_count, _, group_count, group_portion, _ = grouped.shape
    inverse = 1.0 / math.sqrt(HEAD_SIZE)

    def update(running, key_block, value_block, block_positions):
        run_max, run_total, accumulated = running
        block_length = key_block.shape[0]
        heads_of_keys = key_block.reshape(block_length, group_count, HEAD_SIZE)
        heads_of_values = value_block.reshape(block_length, slot_count, group_count, HEAD_SIZE)
        scores = (
            jnp.einsum(
                "rsgjd,kgd->sgjrk", grouped, heads_of_keys, preferred_element_type=jnp.float32
            )
            * inverse
        )
        visible = (block_positions[None, :] <= positions[:, None]) & (
            block_positions[None, :] < live_length
        )
        masked = jnp.where(visible, scores, -1e30)
        new_max = jnp.maximum(run_max, jnp.max(masked, axis=-1))
        weights = jnp.where(visible, jnp.exp(masked - new_max[..., None]), 0.0)
        factor = jnp.exp(run_max - new_max)
        new_total = run_total * factor + jnp.sum(weights, axis=-1)
        new_accumulated = accumulated * factor[..., None] + jnp.einsum(
            "sgjrk,ksgd->sgjrd",
            weights.astype(jnp.bfloat16),
            heads_of_values,
            preferred_element_type=jnp.float32,
        )
        return (new_max, new_total, new_accumulated)

    initial = (
        jnp.full((slot_count, group_count, group_portion, row_count), -1e30, jnp.float32),
        jnp.zeros((slot_count, group_count, group_portion, row_count), jnp.float32),
        jnp.zeros((slot_count, group_count, group_portion, row_count, HEAD_SIZE), jnp.float32),
    )
    piece_rows = keys.shape[0]
    step_rows = block_rows(piece_rows)

    def advance(block_index, current):
        offset = block_index * step_rows
        key_block = lax.dynamic_slice_in_dim(keys, offset, step_rows, 0)
        value_block = lax.dynamic_slice_in_dim(values, offset, step_rows, 0)
        block_positions = lax.dynamic_slice_in_dim(key_positions, offset, step_rows, 0)
        return update(current, key_block, value_block, block_positions)

    run_max, run_total, accumulated = lax.fori_loop(0, piece_rows // step_rows, advance, initial)
    result = accumulated / run_total[..., None]
    return (
        jnp.transpose(result, (0, 3, 1, 2, 4))
        .reshape(slot_count, row_count, group_count * group_portion * HEAD_SIZE)
        .astype(jnp.bfloat16)
    )


def per_device(
    activations,
    query_base,
    key_base,
    plain_value_rows,
    query_down,
    query_up,
    value_down,
    value_raise_factor,
    member_lists,
    prompt_lengths,
):
    row_count = activations.shape[1]
    member_ids = member_lists[0]
    slot_count = member_ids.shape[0]
    up_width = query_up.shape[2]
    group_count = key_base.shape[2] // HEAD_SIZE
    ctx = lax.axis_index("ctx")
    positions = ctx * row_count + jnp.arange(row_count, dtype=jnp.int32)
    downs = jnp.stack([query_down, value_down], axis=1)
    ups = jnp.concatenate([query_up, value_raise_factor], axis=2)
    down_half, up_half = select_members((downs, ups), member_ids, member_lists)
    ups = ctx_gather(up_half, 1, False)
    up_query = ups[..., :up_width]
    up_value = ups[..., up_width:]
    if lax.axis_size("ctx") == 2:
        tokens = ctx_gather(activations[0], 0, False)
        partial = jnp.einsum("rd,sfkd->rfsk", tokens, down_half, preferred_element_type=jnp.float32)
        mine = mp_sum(partial).astype(jnp.bfloat16)
        theirs = swap(mine, "ctx", 1)
        theirs = jnp.concatenate([theirs[row_count:], theirs[:row_count]], axis=0)
        ranks = jnp.concatenate([mine, theirs], axis=3)
        value_rows = ctx_gather(plain_value_rows[0], 0, False)
        keys = ctx_gather(key_base[0], 0, False)
        own_keys = jnp.arange(row_count, dtype=jnp.int32)
        key_positions = jnp.concatenate(
            [ctx * row_count + own_keys, (1 - ctx) * row_count + own_keys]
        )
        rank_query = ranks[:row_count, 0]
        rank_value = ranks[:, 1]
    else:
        downs = ctx_gather(down_half, 2, False)
        partial = jnp.einsum(
            "rd,sfkd->rfsk", activations[0], downs, preferred_element_type=jnp.float32
        )
        ranks = mp_sum(partial).astype(jnp.bfloat16)
        rank_query = ranks[:, 0]
        rank_value = ranks[:, 1]
        value_rows = plain_value_rows[0]
        keys = ctx_gather(key_base[0], 0, True)
        key_positions = jnp.arange(keys.shape[0], dtype=jnp.int32)
    query_matrix = (
        query_base[0][:, None, :]
        + jnp.einsum("rsk,skc->rsc", rank_query, up_query, preferred_element_type=jnp.float32)
    ).astype(jnp.bfloat16)
    group_portion = query_matrix.shape[2] // (group_count * HEAD_SIZE)
    grouped = query_matrix.reshape(row_count, slot_count, group_count, group_portion, HEAD_SIZE)
    built = (
        value_rows[:, None, :]
        + jnp.einsum("rsk,skc->rsc", rank_value, up_value, preferred_element_type=jnp.float32)
    ).astype(jnp.bfloat16)
    values = built.reshape(built.shape[0], slot_count * group_count * HEAD_SIZE)
    if lax.axis_size("ctx") != 2:
        values = ctx_gather(values, 0, True)
    result = attend(
        grouped, keys, values, key_positions, positions, prompt_lengths[0], slot_count
    )
    return result[:, None]


def solution(mesh):
    in_specs = (
        P("req", "ctx", "mp"),
        P("req", "ctx", "mp"),
        P("req", "ctx", "mp"),
        P("req", "ctx", "mp"),
        P("req", "ctx", "mp"),
        P("req", "ctx", "mp"),
        P("req", "ctx", "mp"),
        P("req", "ctx", "mp"),
        P("req", None),
        P("req"),
    )
    out_specs = P(None, "req", "ctx", "mp")
    return jax.shard_map(
        per_device, mesh=mesh, in_specs=in_specs, out_specs=out_specs, check_vma=False
    )
```

```python
import math

import jax
import jax.numpy as jnp
from jax import lax
from jax.sharding import PartitionSpec as P

HEAD_SIZE = 128


def block_rows(total_rows):
    if total_rows <= 512:
        return total_rows
    for candidate in range(512, 0, -1):
        if total_rows % candidate == 0:
            return candidate
    return total_rows


def swap(value, axis, bit):
    size = lax.axis_size(axis)
    return lax.ppermute(value, axis, [(i, i ^ bit) for i in range(size)])


def ctx_gather(mine, dim, ordered):
    if lax.axis_size("ctx") == 2:
        other = swap(mine, "ctx", 1)
        if not ordered:
            return jnp.concatenate([mine, other], axis=dim)
        first = lax.axis_index("ctx") == 0
        low = jnp.where(first, mine, other)
        high = jnp.where(first, other, mine)
        return jnp.concatenate([low, high], axis=dim)
    return lax.all_gather(mine, "ctx", axis=dim, tiled=True)


def mp_sum(value):
    size = lax.axis_size("mp")
    if size & (size - 1):
        return lax.psum(value, "mp")
    sent = value.astype(jnp.bfloat16)
    total = value
    for bit in range(1, size):
        total = total + swap(sent, "mp", bit).astype(jnp.float32)
    return total


def select_members(factor_set, member_ids, member_lists):
    local_count = factor_set[0].shape[0]
    req_size = lax.axis_size("req")
    if req_size != 4:
        everything = [lax.all_gather(f, "req", axis=0, tiled=True) for f in factor_set]
        return [
            jnp.stack([lax.dynamic_index_in_dim(f, m, 0, keepdims=False) for m in member_ids])
            for f in everything
        ]
    req = lax.axis_index("req")
    core = req % 2
    row = req // 2
    row_span = 2 * local_count
    far_ids = swap(member_lists, "req", 2)[0]

    def pick(own, partner, index):
        mine = lax.dynamic_index_in_dim(own, index % local_count, 0, keepdims=False)
        theirs = lax.dynamic_index_in_dim(partner, index % local_count, 0, keepdims=False)
        return jnp.where(index // local_count == core, mine, theirs)

    partners = []
    incoming = []
    previous = None
    for own in factor_set:
        if previous is not None:
            own = lax.optimization_barrier((own, previous[0]))[0]
        partner = swap(own, "req", 1)
        outgoing = jnp.stack(
            [pick(own, partner, far_ids[s] % row_span) for s in range(far_ids.shape[0])]
        )
        if previous is not None:
            outgoing = lax.optimization_barrier((outgoing, previous[1]))[0]
        received = swap(outgoing, "req", 2)
        partners.append(partner)
        incoming.append(received)
        previous = (partner, received)
    chosen = []
    for own, partner, received in zip(factor_set, partners, incoming):
        slots = []
        for s in range(member_ids.shape[0]):
            m = member_ids[s]
            near = pick(own, partner, m % row_span)
            slots.append(jnp.where(m // row_span == row, near, received[s]))
        chosen.append(jnp.stack(slots))
    return chosen


def attend(grouped, keys, values, key_positions, positions, live_length, slot_count):
    row_count, _, group_count, group_portion, _ = grouped.shape
    inverse = 1.0 / math.sqrt(HEAD_SIZE)

    def update(running, key_block, value_block, block_positions):
        run_max, run_total, accumulated = running
        block_length = key_block.shape[0]
        heads_of_keys = key_block.reshape(block_length, group_count, HEAD_SIZE)
        heads_of_values = value_block.reshape(block_length, slot_count, group_count, HEAD_SIZE)
        scores = (
            jnp.einsum(
                "rsgjd,kgd->sgjrk", grouped, heads_of_keys, preferred_element_type=jnp.float32
            )
            * inverse
        )
        visible = (block_positions[None, :] <= positions[:, None]) & (
            block_positions[None, :] < live_length
        )
        masked = jnp.where(visible, scores, -1e30)
        new_max = jnp.maximum(run_max, jnp.max(masked, axis=-1))
        weights = jnp.where(visible, jnp.exp(masked - new_max[..., None]), 0.0)
        factor = jnp.exp(run_max - new_max)
        new_total = run_total * factor + jnp.sum(weights, axis=-1)
        new_accumulated = accumulated * factor[..., None] + jnp.einsum(
            "sgjrk,ksgd->sgjrd",
            weights.astype(jnp.bfloat16),
            heads_of_values,
            preferred_element_type=jnp.float32,
        )
        return (new_max, new_total, new_accumulated)

    initial = (
        jnp.full((slot_count, group_count, group_portion, row_count), -1e30, jnp.float32),
        jnp.zeros((slot_count, group_count, group_portion, row_count), jnp.float32),
        jnp.zeros((slot_count, group_count, group_portion, row_count, HEAD_SIZE), jnp.float32),
    )
    piece_rows = keys.shape[0]
    step_rows = block_rows(piece_rows)

    def advance(block_index, current):
        offset = block_index * step_rows
        key_block = lax.dynamic_slice_in_dim(keys, offset, step_rows, 0)
        value_block = lax.dynamic_slice_in_dim(values, offset, step_rows, 0)
        block_positions = lax.dynamic_slice_in_dim(key_positions, offset, step_rows, 0)
        return update(current, key_block, value_block, block_positions)

    run_max, run_total, accumulated = lax.fori_loop(0, piece_rows // step_rows, advance, initial)
    result = accumulated / run_total[..., None]
    return (
        jnp.transpose(result, (0, 3, 1, 2, 4))
        .reshape(slot_count, row_count, group_count * group_portion * HEAD_SIZE)
        .astype(jnp.bfloat16)
    )


def per_device(
    activations,
    query_base,
    key_base,
    plain_value_rows,
    query_down,
    query_up,
    value_down,
    value_raise_factor,
    member_lists,
    prompt_lengths,
):
    row_count = activations.shape[1]
    member_ids = member_lists[0]
    slot_count = member_ids.shape[0]
    up_width = query_up.shape[2]
    group_count = key_base.shape[2] // HEAD_SIZE
    ctx = lax.axis_index("ctx")
    positions = ctx * row_count + jnp.arange(row_count, dtype=jnp.int32)
    downs = jnp.stack([query_down, value_down], axis=1)
    ups = jnp.concatenate([query_up, value_raise_factor], axis=2)
    down_half, up_half = select_members((downs, ups), member_ids, member_lists)
    ups = ctx_gather(up_half, 1, False)
    up_query = ups[..., :up_width]
    up_value = ups[..., up_width:]
    if lax.axis_size("ctx") == 2:
        tokens = ctx_gather(activations[0], 0, False)
        partial = jnp.einsum("rd,sfkd->rfsk", tokens, down_half, preferred_element_type=jnp.float32)
        mine = mp_sum(partial).astype(jnp.bfloat16)
        theirs = swap(mine, "ctx", 1)
        theirs = jnp.concatenate([theirs[row_count:], theirs[:row_count]], axis=0)
        ranks = jnp.concatenate([mine, theirs], axis=3)
        value_rows = ctx_gather(plain_value_rows[0], 0, False)
        keys = ctx_gather(key_base[0], 0, False)
        own_keys = jnp.arange(row_count, dtype=jnp.int32)
        key_positions = jnp.concatenate(
            [ctx * row_count + own_keys, (1 - ctx) * row_count + own_keys]
        )
        rank_query = ranks[:row_count, 0]
        rank_value = ranks[:, 1]
    else:
        downs = ctx_gather(down_half, 2, False)
        partial = jnp.einsum(
            "rd,sfkd->rfsk", activations[0], downs, preferred_element_type=jnp.float32
        )
        ranks = mp_sum(partial).astype(jnp.bfloat16)
        rank_query = ranks[:, 0]
        rank_value = ranks[:, 1]
        value_rows = plain_value_rows[0]
        keys = ctx_gather(key_base[0], 0, True)
        key_positions = jnp.arange(keys.shape[0], dtype=jnp.int32)
    query_matrix = (
        query_base[0][:, None, :]
        + jnp.einsum("rsk,skc->rsc", rank_query, up_query, preferred_element_type=jnp.float32)
    ).astype(jnp.bfloat16)
    group_portion = query_matrix.shape[2] // (group_count * HEAD_SIZE)
    grouped = query_matrix.reshape(row_count, slot_count, group_count, group_portion, HEAD_SIZE)
    built = (
        value_rows[:, None, :]
        + jnp.einsum("rsk,skc->rsc", rank_value, up_value, preferred_element_type=jnp.float32)
    ).astype(jnp.bfloat16)
    values = built.reshape(built.shape[0], slot_count * group_count * HEAD_SIZE)
    if lax.axis_size("ctx") != 2:
        values = ctx_gather(values, 0, True)
    result = attend(
        grouped, keys, values, key_positions, positions, prompt_lengths[0], slot_count
    )
    return result[:, None]


def solution(mesh):
    in_specs = (
        P("req", "ctx", "mp"),
        P("req", "ctx", "mp"),
        P("req", "ctx", "mp"),
        P("req", "ctx", "mp"),
        P("req", "ctx", "mp"),
        P("req", "ctx", "mp"),
        P("req", "ctx", "mp"),
        P("req", "ctx", "mp"),
        P("req", None),
        P("req"),
    )
    out_specs = P(None, "req", "ctx", "mp")
    return jax.shard_map(
        per_device, mesh=mesh, in_specs=in_specs, out_specs=out_specs, check_vma=False
    )
```

```python
import math

import jax
import jax.numpy as jnp
from jax import lax
from jax.sharding import PartitionSpec as P

HEAD_SIZE = 128


def block_rows(total_rows):
    if total_rows <= 512:
        return total_rows
    for candidate in range(512, 0, -1):
        if total_rows % candidate == 0:
            return candidate
    return total_rows


def swap(value, axis, bit):
    size = lax.axis_size(axis)
    return lax.ppermute(value, axis, [(i, i ^ bit) for i in range(size)])


def ctx_gather(mine, dim, ordered):
    if lax.axis_size("ctx") == 2:
        other = swap(mine, "ctx", 1)
        if not ordered:
            return jnp.concatenate([mine, other], axis=dim)
        first = lax.axis_index("ctx") == 0
        low = jnp.where(first, mine, other)
        high = jnp.where(first, other, mine)
        return jnp.concatenate([low, high], axis=dim)
    return lax.all_gather(mine, "ctx", axis=dim, tiled=True)


def mp_sum(value):
    size = lax.axis_size("mp")
    if size & (size - 1):
        return lax.psum(value, "mp")
    total = value
    for bit in range(1, size):
        total = total + swap(value, "mp", bit)
    return total


def select_members(factor_set, member_ids, member_lists):
    local_count = factor_set[0].shape[0]
    req_size = lax.axis_size("req")
    if req_size != 4:
        everything = [lax.all_gather(f, "req", axis=0, tiled=True) for f in factor_set]
        return [
            jnp.stack([lax.dynamic_index_in_dim(f, m, 0, keepdims=False) for m in member_ids])
            for f in everything
        ], everything[0]
    req = lax.axis_index("req")
    core = req % 2
    row = req // 2
    row_span = 2 * local_count
    far_ids = swap(member_lists, "req", 2)[0]

    def pick(own, partner, index):
        mine = lax.dynamic_index_in_dim(own, index % local_count, 0, keepdims=False)
        theirs = lax.dynamic_index_in_dim(partner, index % local_count, 0, keepdims=False)
        return jnp.where(index // local_count == core, mine, theirs)

    partners = []
    incoming = []
    previous = None
    for own in factor_set:
        if previous is not None:
            own = lax.optimization_barrier((own, previous[0]))[0]
        partner = swap(own, "req", 1)
        outgoing = jnp.stack(
            [pick(own, partner, far_ids[s] % row_span) for s in range(far_ids.shape[0])]
        )
        if previous is not None:
            outgoing = lax.optimization_barrier((outgoing, previous[1]))[0]
        received = swap(outgoing, "req", 2)
        partners.append(partner)
        incoming.append(received)
        previous = (partner, received)
    chosen = []
    for own, partner, received in zip(factor_set, partners, incoming):
        slots = []
        for s in range(member_ids.shape[0]):
            m = member_ids[s]
            near = pick(own, partner, m % row_span)
            slots.append(jnp.where(m // row_span == row, near, received[s]))
        chosen.append(jnp.stack(slots))
    return chosen, partners[0]


def attend(grouped, keys, values, key_positions, positions, live_length, slot_count):
    row_count, _, group_count, group_portion, _ = grouped.shape
    inverse = 1.0 / math.sqrt(HEAD_SIZE)

    def update(running, key_block, value_block, block_positions):
        run_max, run_total, accumulated = running
        block_length = key_block.shape[0]
        heads_of_keys = key_block.reshape(block_length, group_count, HEAD_SIZE)
        heads_of_values = value_block.reshape(block_length, slot_count, group_count, HEAD_SIZE)
        scores = (
            jnp.einsum(
                "rsgjd,kgd->sgjrk", grouped, heads_of_keys, preferred_element_type=jnp.float32
            )
            * inverse
        )
        visible = (block_positions[None, :] <= positions[:, None]) & (
            block_positions[None, :] < live_length
        )
        masked = jnp.where(visible, scores, -1e30)
        new_max = jnp.maximum(run_max, jnp.max(masked, axis=-1))
        weights = jnp.where(visible, jnp.exp(masked - new_max[..., None]), 0.0)
        factor = jnp.exp(run_max - new_max)
        new_total = run_total * factor + jnp.sum(weights, axis=-1)
        new_accumulated = accumulated * factor[..., None] + jnp.einsum(
            "sgjrk,ksgd->sgjrd",
            weights.astype(jnp.bfloat16),
            heads_of_values,
            preferred_element_type=jnp.float32,
        )
        return (new_max, new_total, new_accumulated)

    initial = (
        jnp.full((slot_count, group_count, group_portion, row_count), -1e30, jnp.float32),
        jnp.zeros((slot_count, group_count, group_portion, row_count), jnp.float32),
        jnp.zeros((slot_count, group_count, group_portion, row_count, HEAD_SIZE), jnp.float32),
    )
    piece_rows = keys.shape[0]
    step_rows = block_rows(piece_rows)

    def advance(block_index, current):
        offset = block_index * step_rows
        key_block = lax.dynamic_slice_in_dim(keys, offset, step_rows, 0)
        value_block = lax.dynamic_slice_in_dim(values, offset, step_rows, 0)
        block_positions = lax.dynamic_slice_in_dim(key_positions, offset, step_rows, 0)
        return update(current, key_block, value_block, block_positions)

    run_max, run_total, accumulated = lax.fori_loop(0, piece_rows // step_rows, advance, initial)
    result = accumulated / run_total[..., None]
    return (
        jnp.transpose(result, (0, 3, 1, 2, 4))
        .reshape(slot_count, row_count, group_count * group_portion * HEAD_SIZE)
        .astype(jnp.bfloat16)
    )


def per_device(
    activations,
    query_base,
    key_base,
    plain_value_rows,
    query_down,
    query_up,
    value_down,
    value_raise_factor,
    member_lists,
    prompt_lengths,
):
    row_count = activations.shape[1]
    member_ids = member_lists[0]
    slot_count = member_ids.shape[0]
    up_width = query_up.shape[2]
    group_count = key_base.shape[2] // HEAD_SIZE
    ctx = lax.axis_index("ctx")
    positions = ctx * row_count + jnp.arange(row_count, dtype=jnp.int32)
    downs = jnp.stack([query_down, value_down], axis=1)
    ups = jnp.concatenate([query_up, value_raise_factor], axis=2)
    (down_half, up_half), first = select_members((downs, ups), member_ids, member_lists)
    ups = ctx_gather(up_half, 1, False)
    up_query = ups[..., :up_width]
    up_value = ups[..., up_width:]
    if lax.axis_size("ctx") == 2:
        local_rows, value_rows, keys, _ = lax.optimization_barrier(
            (activations[0], plain_value_rows[0], key_base[0], first)
        )
        tokens = ctx_gather(local_rows, 0, False)
        partial = jnp.einsum("rd,sfkd->rfsk", tokens, down_half, preferred_element_type=jnp.float32)
        mine = mp_sum(partial).astype(jnp.bfloat16)
        theirs = swap(mine, "ctx", 1)
        theirs = jnp.concatenate([theirs[row_count:], theirs[:row_count]], axis=0)
        ranks = jnp.concatenate([mine, theirs], axis=3)
        value_rows = ctx_gather(value_rows, 0, False)
        keys = ctx_gather(keys, 0, False)
        own_keys = jnp.arange(row_count, dtype=jnp.int32)
        key_positions = jnp.concatenate(
            [ctx * row_count + own_keys, (1 - ctx) * row_count + own_keys]
        )
        rank_query = ranks[:row_count, 0]
        rank_value = ranks[:, 1]
    else:
        downs = ctx_gather(down_half, 2, False)
        partial = jnp.einsum(
            "rd,sfkd->rfsk", activations[0], downs, preferred_element_type=jnp.float32
        )
        ranks = mp_sum(partial).astype(jnp.bfloat16)
        rank_query = ranks[:, 0]
        rank_value = ranks[:, 1]
        value_rows = plain_value_rows[0]
        keys = ctx_gather(key_base[0], 0, True)
        key_positions = jnp.arange(keys.shape[0], dtype=jnp.int32)
    query_matrix = (
        query_base[0][:, None, :]
        + jnp.einsum("rsk,skc->rsc", rank_query, up_query, preferred_element_type=jnp.float32)
    ).astype(jnp.bfloat16)
    group_portion = query_matrix.shape[2] // (group_count * HEAD_SIZE)
    grouped = query_matrix.reshape(row_count, slot_count, group_count, group_portion, HEAD_SIZE)
    built = (
        value_rows[:, None, :]
        + jnp.einsum("rsk,skc->rsc", rank_value, up_value, preferred_element_type=jnp.float32)
    ).astype(jnp.bfloat16)
    values = built.reshape(built.shape[0], slot_count * group_count * HEAD_SIZE)
    if lax.axis_size("ctx") != 2:
        values = ctx_gather(values, 0, True)
    result = attend(
        grouped, keys, values, key_positions, positions, prompt_lengths[0], slot_count
    )
    return result[:, None]


def solution(mesh):
    in_specs = (
        P("req", "ctx", "mp"),
        P("req", "ctx", "mp"),
        P("req", "ctx", "mp"),
        P("req", "ctx", "mp"),
        P("req", "ctx", "mp"),
        P("req", "ctx", "mp"),
        P("req", "ctx", "mp"),
        P("req", "ctx", "mp"),
        P("req", None),
        P("req"),
    )
    out_specs = P(None, "req", "ctx", "mp")
    return jax.shard_map(
        per_device, mesh=mesh, in_specs=in_specs, out_specs=out_specs, check_vma=False
    )
```

```python
import math

import jax
import jax.numpy as jnp
from jax import lax
from jax.sharding import PartitionSpec as P

HEAD_SIZE = 128


def block_rows(total_rows):
    if total_rows <= 512:
        return total_rows
    for candidate in range(512, 0, -1):
        if total_rows % candidate == 0:
            return candidate
    return total_rows


def swap(value, axis, bit):
    size = lax.axis_size(axis)
    return lax.ppermute(value, axis, [(i, i ^ bit) for i in range(size)])


def ctx_gather(mine, dim, ordered):
    if lax.axis_size("ctx") == 2:
        other = swap(mine, "ctx", 1)
        if not ordered:
            return jnp.concatenate([mine, other], axis=dim)
        first = lax.axis_index("ctx") == 0
        low = jnp.where(first, mine, other)
        high = jnp.where(first, other, mine)
        return jnp.concatenate([low, high], axis=dim)
    return lax.all_gather(mine, "ctx", axis=dim, tiled=True)


def mp_sum(value):
    size = lax.axis_size("mp")
    if size & (size - 1):
        return lax.psum(value, "mp")
    total = value
    for bit in range(1, size):
        total = total + swap(value, "mp", bit)
    return total


def select_members(factor_set, member_ids, member_lists):
    local_count = factor_set[0].shape[0]
    req_size = lax.axis_size("req")
    if req_size != 4:
        everything = [lax.all_gather(f, "req", axis=0, tiled=True) for f in factor_set]
        return [
            jnp.stack([lax.dynamic_index_in_dim(f, m, 0, keepdims=False) for m in member_ids])
            for f in everything
        ], everything[0]
    req = lax.axis_index("req")
    core = req % 2
    row = req // 2
    row_span = 2 * local_count
    far_ids = swap(member_lists, "req", 2)[0]

    def pick(own, partner, index):
        mine = lax.dynamic_index_in_dim(own, index % local_count, 0, keepdims=False)
        theirs = lax.dynamic_index_in_dim(partner, index % local_count, 0, keepdims=False)
        return jnp.where(index // local_count == core, mine, theirs)

    partners = []
    incoming = []
    previous = None
    for own in factor_set:
        if previous is not None:
            own = lax.optimization_barrier((own, previous[0]))[0]
        partner = swap(own, "req", 1)
        outgoing = jnp.stack(
            [pick(own, partner, far_ids[s] % row_span) for s in range(far_ids.shape[0])]
        )
        if previous is not None:
            outgoing = lax.optimization_barrier((outgoing, previous[1]))[0]
        received = swap(outgoing, "req", 2)
        partners.append(partner)
        incoming.append(received)
        previous = (partner, received)
    chosen = []
    for own, partner, received in zip(factor_set, partners, incoming):
        slots = []
        for s in range(member_ids.shape[0]):
            m = member_ids[s]
            near = pick(own, partner, m % row_span)
            slots.append(jnp.where(m // row_span == row, near, received[s]))
        chosen.append(jnp.stack(slots))
    return chosen, partners[0]


def attend(grouped, keys, values, key_positions, positions, live_length, slot_count):
    row_count, _, group_count, group_portion, _ = grouped.shape
    inverse = 1.0 / math.sqrt(HEAD_SIZE)

    def update(running, key_block, value_block, block_positions):
        run_max, run_total, accumulated = running
        block_length = key_block.shape[0]
        heads_of_keys = key_block.reshape(block_length, group_count, HEAD_SIZE)
        heads_of_values = value_block.reshape(block_length, slot_count, group_count, HEAD_SIZE)
        scores = (
            jnp.einsum(
                "rsgjd,kgd->sgjrk", grouped, heads_of_keys, preferred_element_type=jnp.float32
            )
            * inverse
        )
        visible = (block_positions[None, :] <= positions[:, None]) & (
            block_positions[None, :] < live_length
        )
        masked = jnp.where(visible, scores, -1e30)
        new_max = jnp.maximum(run_max, jnp.max(masked, axis=-1))
        weights = jnp.where(visible, jnp.exp(masked - new_max[..., None]), 0.0)
        factor = jnp.exp(run_max - new_max)
        new_total = run_total * factor + jnp.sum(weights, axis=-1)
        new_accumulated = accumulated * factor[..., None] + jnp.einsum(
            "sgjrk,ksgd->sgjrd",
            weights.astype(jnp.bfloat16),
            heads_of_values,
            preferred_element_type=jnp.float32,
        )
        return (new_max, new_total, new_accumulated)

    initial = (
        jnp.full((slot_count, group_count, group_portion, row_count), -1e30, jnp.float32),
        jnp.zeros((slot_count, group_count, group_portion, row_count), jnp.float32),
        jnp.zeros((slot_count, group_count, group_portion, row_count, HEAD_SIZE), jnp.float32),
    )
    piece_rows = keys.shape[0]
    step_rows = block_rows(piece_rows)

    def advance(block_index, current):
        offset = block_index * step_rows
        key_block = lax.dynamic_slice_in_dim(keys, offset, step_rows, 0)
        value_block = lax.dynamic_slice_in_dim(values, offset, step_rows, 0)
        block_positions = lax.dynamic_slice_in_dim(key_positions, offset, step_rows, 0)
        return update(current, key_block, value_block, block_positions)

    run_max, run_total, accumulated = lax.fori_loop(0, piece_rows // step_rows, advance, initial)
    result = accumulated / run_total[..., None]
    return (
        jnp.transpose(result, (0, 3, 1, 2, 4))
        .reshape(slot_count, row_count, group_count * group_portion * HEAD_SIZE)
        .astype(jnp.bfloat16)
    )


def per_device(
    activations,
    query_base,
    key_base,
    plain_value_rows,
    query_down,
    query_up,
    value_down,
    value_raise_factor,
    member_lists,
    prompt_lengths,
):
    row_count = activations.shape[1]
    member_ids = member_lists[0]
    slot_count = member_ids.shape[0]
    up_width = query_up.shape[2]
    group_count = key_base.shape[2] // HEAD_SIZE
    ctx = lax.axis_index("ctx")
    positions = ctx * row_count + jnp.arange(row_count, dtype=jnp.int32)
    downs = jnp.stack([query_down, value_down], axis=1)
    ups = jnp.concatenate([query_up, value_raise_factor], axis=2)
    (down_half, up_half), first = select_members((downs, ups), member_ids, member_lists)
    ups = ctx_gather(up_half, 1, False)
    up_query = ups[..., :up_width]
    up_value = ups[..., up_width:]
    if lax.axis_size("ctx") == 2:
        local_rows, value_rows, keys, _ = lax.optimization_barrier(
            (activations[0], plain_value_rows[0], key_base[0], first)
        )
        tokens = ctx_gather(local_rows, 0, False)
        partial = jnp.einsum("rd,sfkd->rfsk", tokens, down_half, preferred_element_type=jnp.float32)
        mine = lax.psum(partial, "mp").astype(jnp.bfloat16)
        theirs = swap(mine, "ctx", 1)
        theirs = jnp.concatenate([theirs[row_count:], theirs[:row_count]], axis=0)
        ranks = jnp.concatenate([mine, theirs], axis=3)
        value_rows = ctx_gather(value_rows, 0, False)
        keys = ctx_gather(keys, 0, False)
        own_keys = jnp.arange(row_count, dtype=jnp.int32)
        key_positions = jnp.concatenate(
            [ctx * row_count + own_keys, (1 - ctx) * row_count + own_keys]
        )
        rank_query = ranks[:row_count, 0]
        rank_value = ranks[:, 1]
    else:
        downs = ctx_gather(down_half, 2, False)
        partial = jnp.einsum(
            "rd,sfkd->rfsk", activations[0], downs, preferred_element_type=jnp.float32
        )
        ranks = mp_sum(partial).astype(jnp.bfloat16)
        rank_query = ranks[:, 0]
        rank_value = ranks[:, 1]
        value_rows = plain_value_rows[0]
        keys = ctx_gather(key_base[0], 0, True)
        key_positions = jnp.arange(keys.shape[0], dtype=jnp.int32)
    query_matrix = (
        query_base[0][:, None, :]
        + jnp.einsum("rsk,skc->rsc", rank_query, up_query, preferred_element_type=jnp.float32)
    ).astype(jnp.bfloat16)
    group_portion = query_matrix.shape[2] // (group_count * HEAD_SIZE)
    grouped = query_matrix.reshape(row_count, slot_count, group_count, group_portion, HEAD_SIZE)
    built = (
        value_rows[:, None, :]
        + jnp.einsum("rsk,skc->rsc", rank_value, up_value, preferred_element_type=jnp.float32)
    ).astype(jnp.bfloat16)
    values = built.reshape(built.shape[0], slot_count * group_count * HEAD_SIZE)
    if lax.axis_size("ctx") != 2:
        values = ctx_gather(values, 0, True)
    result = attend(
        grouped, keys, values, key_positions, positions, prompt_lengths[0], slot_count
    )
    return result[:, None]


def solution(mesh):
    in_specs = (
        P("req", "ctx", "mp"),
        P("req", "ctx", "mp"),
        P("req", "ctx", "mp"),
        P("req", "ctx", "mp"),
        P("req", "ctx", "mp"),
        P("req", "ctx", "mp"),
        P("req", "ctx", "mp"),
        P("req", "ctx", "mp"),
        P("req", None),
        P("req"),
    )
    out_specs = P(None, "req", "ctx", "mp")
    return jax.shard_map(
        per_device, mesh=mesh, in_specs=in_specs, out_specs=out_specs, check_vma=False
    )
```

```python
import math

import jax
import jax.numpy as jnp
from jax import lax
from jax.sharding import PartitionSpec as P

HEAD_SIZE = 128


def block_rows(total_rows):
    if total_rows <= 512:
        return total_rows
    for candidate in range(512, 0, -1):
        if total_rows % candidate == 0:
            return candidate
    return total_rows


def swap(value, axis, bit):
    size = lax.axis_size(axis)
    return lax.ppermute(value, axis, [(i, i ^ bit) for i in range(size)])


def ctx_gather(mine, dim, ordered):
    if lax.axis_size("ctx") == 2:
        other = swap(mine, "ctx", 1)
        if not ordered:
            return jnp.concatenate([mine, other], axis=dim)
        first = lax.axis_index("ctx") == 0
        low = jnp.where(first, mine, other)
        high = jnp.where(first, other, mine)
        return jnp.concatenate([low, high], axis=dim)
    return lax.all_gather(mine, "ctx", axis=dim, tiled=True)


def mp_sum(value):
    size = lax.axis_size("mp")
    if size & (size - 1):
        return lax.psum(value, "mp")
    total = value
    for bit in range(1, size):
        total = total + swap(value, "mp", bit)
    return total


def select_members(factor_set, member_ids, member_lists):
    local_count = factor_set[0].shape[0]
    req_size = lax.axis_size("req")
    if req_size != 4:
        everything = [lax.all_gather(f, "req", axis=0, tiled=True) for f in factor_set]
        return [
            jnp.stack([lax.dynamic_index_in_dim(f, m, 0, keepdims=False) for m in member_ids])
            for f in everything
        ], everything[0]
    req = lax.axis_index("req")
    core = req % 2
    row = req // 2
    row_span = 2 * local_count
    far_ids = swap(member_lists, "req", 2)[0]

    def pick(own, partner, index):
        mine = lax.dynamic_index_in_dim(own, index % local_count, 0, keepdims=False)
        theirs = lax.dynamic_index_in_dim(partner, index % local_count, 0, keepdims=False)
        return jnp.where(index // local_count == core, mine, theirs)

    partners = []
    incoming = []
    previous = None
    for own in factor_set:
        if previous is not None:
            own = lax.optimization_barrier((own, previous[0]))[0]
        partner = swap(own, "req", 1)
        outgoing = jnp.stack(
            [pick(own, partner, far_ids[s] % row_span) for s in range(far_ids.shape[0])]
        )
        if previous is not None:
            outgoing = lax.optimization_barrier((outgoing, previous[1]))[0]
        received = swap(outgoing, "req", 2)
        partners.append(partner)
        incoming.append(received)
        previous = (partner, received)
    chosen = []
    for own, partner, received in zip(factor_set, partners, incoming):
        slots = []
        for s in range(member_ids.shape[0]):
            m = member_ids[s]
            near = pick(own, partner, m % row_span)
            slots.append(jnp.where(m // row_span == row, near, received[s]))
        chosen.append(jnp.stack(slots))
    return chosen, partners[0]


def attend(grouped, keys, values, key_positions, positions, live_length, slot_count):
    row_count, _, group_count, group_portion, _ = grouped.shape
    inverse = 1.0 / math.sqrt(HEAD_SIZE)

    def update(running, key_block, value_block, block_positions):
        run_max, run_total, accumulated = running
        block_length = key_block.shape[0]
        heads_of_keys = key_block.reshape(block_length, group_count, HEAD_SIZE)
        heads_of_values = value_block.reshape(block_length, slot_count, group_count, HEAD_SIZE)
        scores = (
            jnp.einsum(
                "rsgjd,kgd->sgjrk", grouped, heads_of_keys, preferred_element_type=jnp.float32
            )
            * inverse
        )
        visible = (block_positions[None, :] <= positions[:, None]) & (
            block_positions[None, :] < live_length
        )
        masked = jnp.where(visible, scores, -1e30)
        new_max = jnp.maximum(run_max, jnp.max(masked, axis=-1))
        weights = jnp.where(visible, jnp.exp(masked - new_max[..., None]), 0.0)
        factor = jnp.exp(run_max - new_max)
        new_total = run_total * factor + jnp.sum(weights, axis=-1)
        new_accumulated = accumulated * factor[..., None] + jnp.einsum(
            "sgjrk,ksgd->sgjrd",
            weights.astype(jnp.bfloat16),
            heads_of_values,
            preferred_element_type=jnp.float32,
        )
        return (new_max, new_total, new_accumulated)

    initial = (
        jnp.full((slot_count, group_count, group_portion, row_count), -1e30, jnp.float32),
        jnp.zeros((slot_count, group_count, group_portion, row_count), jnp.float32),
        jnp.zeros((slot_count, group_count, group_portion, row_count, HEAD_SIZE), jnp.float32),
    )
    piece_rows = keys.shape[0]
    step_rows = block_rows(piece_rows)

    def advance(block_index, current):
        offset = block_index * step_rows
        key_block = lax.dynamic_slice_in_dim(keys, offset, step_rows, 0)
        value_block = lax.dynamic_slice_in_dim(values, offset, step_rows, 0)
        block_positions = lax.dynamic_slice_in_dim(key_positions, offset, step_rows, 0)
        return update(current, key_block, value_block, block_positions)

    run_max, run_total, accumulated = lax.fori_loop(0, piece_rows // step_rows, advance, initial)
    result = accumulated / run_total[..., None]
    return (
        jnp.transpose(result, (0, 3, 1, 2, 4))
        .reshape(slot_count, row_count, group_count * group_portion * HEAD_SIZE)
        .astype(jnp.bfloat16)
    )


def per_device(
    activations,
    query_base,
    key_base,
    plain_value_rows,
    query_down,
    query_up,
    value_down,
    value_raise_factor,
    member_lists,
    prompt_lengths,
):
    row_count = activations.shape[1]
    member_ids = member_lists[0]
    slot_count = member_ids.shape[0]
    up_width = query_up.shape[2]
    group_count = key_base.shape[2] // HEAD_SIZE
    ctx = lax.axis_index("ctx")
    positions = ctx * row_count + jnp.arange(row_count, dtype=jnp.int32)
    downs = jnp.stack([query_down, value_down], axis=1)
    ups = jnp.concatenate([query_up, value_raise_factor], axis=2)
    early = lax.axis_size("ctx") == 2
    if early:
        ups = ctx_gather(ups, 1, False)
    (down_half, up_half), first = select_members((downs, ups), member_ids, member_lists)
    ups = up_half if early else ctx_gather(up_half, 1, False)
    up_query = ups[..., :up_width]
    up_value = ups[..., up_width:]
    if lax.axis_size("ctx") == 2:
        local_rows, value_rows, keys, _ = lax.optimization_barrier(
            (activations[0], plain_value_rows[0], key_base[0], first)
        )
        tokens = ctx_gather(local_rows, 0, False)
        partial = jnp.einsum("rd,sfkd->rfsk", tokens, down_half, preferred_element_type=jnp.float32)
        mine = mp_sum(partial).astype(jnp.bfloat16)
        theirs = swap(mine, "ctx", 1)
        theirs = jnp.concatenate([theirs[row_count:], theirs[:row_count]], axis=0)
        ranks = jnp.concatenate([mine, theirs], axis=3)
        value_rows = ctx_gather(value_rows, 0, False)
        keys = ctx_gather(keys, 0, False)
        own_keys = jnp.arange(row_count, dtype=jnp.int32)
        key_positions = jnp.concatenate(
            [ctx * row_count + own_keys, (1 - ctx) * row_count + own_keys]
        )
        rank_query = ranks[:row_count, 0]
        rank_value = ranks[:, 1]
    else:
        downs = ctx_gather(down_half, 2, False)
        partial = jnp.einsum(
            "rd,sfkd->rfsk", activations[0], downs, preferred_element_type=jnp.float32
        )
        ranks = mp_sum(partial).astype(jnp.bfloat16)
        rank_query = ranks[:, 0]
        rank_value = ranks[:, 1]
        value_rows = plain_value_rows[0]
        keys = ctx_gather(key_base[0], 0, True)
        key_positions = jnp.arange(keys.shape[0], dtype=jnp.int32)
    query_matrix = (
        query_base[0][:, None, :]
        + jnp.einsum("rsk,skc->rsc", rank_query, up_query, preferred_element_type=jnp.float32)
    ).astype(jnp.bfloat16)
    group_portion = query_matrix.shape[2] // (group_count * HEAD_SIZE)
    grouped = query_matrix.reshape(row_count, slot_count, group_count, group_portion, HEAD_SIZE)
    built = (
        value_rows[:, None, :]
        + jnp.einsum("rsk,skc->rsc", rank_value, up_value, preferred_element_type=jnp.float32)
    ).astype(jnp.bfloat16)
    values = built.reshape(built.shape[0], slot_count * group_count * HEAD_SIZE)
    if lax.axis_size("ctx") != 2:
        values = ctx_gather(values, 0, True)
    result = attend(
        grouped, keys, values, key_positions, positions, prompt_lengths[0], slot_count
    )
    return result[:, None]


def solution(mesh):
    in_specs = (
        P("req", "ctx", "mp"),
        P("req", "ctx", "mp"),
        P("req", "ctx", "mp"),
        P("req", "ctx", "mp"),
        P("req", "ctx", "mp"),
        P("req", "ctx", "mp"),
        P("req", "ctx", "mp"),
        P("req", "ctx", "mp"),
        P("req", None),
        P("req"),
    )
    out_specs = P(None, "req", "ctx", "mp")
    return jax.shard_map(
        per_device, mesh=mesh, in_specs=in_specs, out_specs=out_specs, check_vma=False
    )
```

```python
import math

import jax
import jax.numpy as jnp
from jax import lax
from jax.sharding import PartitionSpec as P

HEAD_SIZE = 128


def block_rows(total_rows):
    if total_rows <= 512:
        return total_rows
    for candidate in range(512, 0, -1):
        if total_rows % candidate == 0:
            return candidate
    return total_rows


def swap(value, axis, bit):
    size = lax.axis_size(axis)
    return lax.ppermute(value, axis, [(i, i ^ bit) for i in range(size)])


def ctx_gather(mine, dim, ordered):
    if lax.axis_size("ctx") == 2:
        other = swap(mine, "ctx", 1)
        if not ordered:
            return jnp.concatenate([mine, other], axis=dim)
        first = lax.axis_index("ctx") == 0
        low = jnp.where(first, mine, other)
        high = jnp.where(first, other, mine)
        return jnp.concatenate([low, high], axis=dim)
    return lax.all_gather(mine, "ctx", axis=dim, tiled=True)


def mp_sum(value):
    size = lax.axis_size("mp")
    if size & (size - 1):
        return lax.psum(value, "mp")
    total = value
    for bit in range(1, size):
        total = total + swap(value, "mp", bit)
    return total


def select_members(factor_set, member_ids, member_lists):
    leaves = jax.tree.leaves
    local_count = leaves(factor_set[0])[0].shape[0]
    req_size = lax.axis_size("req")
    if req_size != 4:
        def choose(f):
            everything = lax.all_gather(f, "req", axis=0, tiled=True)
            return jnp.stack(
                [lax.dynamic_index_in_dim(everything, m, 0, keepdims=False) for m in member_ids]
            )

        return [jax.tree.map(choose, group) for group in factor_set], factor_set[0]
    req = lax.axis_index("req")
    core = req % 2
    row = req // 2
    row_span = 2 * local_count
    far_ids = swap(member_lists, "req", 2)[0]

    def pick(own, partner, index):
        mine = lax.dynamic_index_in_dim(own, index % local_count, 0, keepdims=False)
        theirs = lax.dynamic_index_in_dim(partner, index % local_count, 0, keepdims=False)
        return jnp.where(index // local_count == core, mine, theirs)

    def picked(own, partner, ids):
        return jax.tree.map(
            lambda o, p: jnp.stack([pick(o, p, ids[s] % row_span) for s in range(ids.shape[0])]),
            own,
            partner,
        )

    partners = []
    incoming = []
    previous = None
    for own in factor_set:
        if previous is not None:
            own = lax.optimization_barrier((own, previous[0]))[0]
        partner = swap(own, "req", 1)
        outgoing = picked(own, partner, far_ids)
        if previous is not None:
            outgoing = lax.optimization_barrier((outgoing, previous[1]))[0]
        received = swap(outgoing, "req", 2)
        partners.append(partner)
        incoming.append(received)
        previous = (partner, received)
    chosen = []
    near_rows = [member_ids[s] // row_span == row for s in range(member_ids.shape[0])]
    for own, partner, received in zip(factor_set, partners, incoming):
        near = picked(own, partner, member_ids)
        chosen.append(
            jax.tree.map(
                lambda n, r: jnp.stack(
                    [jnp.where(near_rows[s], n[s], r[s]) for s in range(len(near_rows))]
                ),
                near,
                received,
            )
        )
    return chosen, partners[0]


def attend(grouped, keys, values, key_positions, positions, live_length, slot_count):
    row_count, _, group_count, group_portion, _ = grouped.shape
    inverse = 1.0 / math.sqrt(HEAD_SIZE)

    def update(running, key_block, value_block, block_positions):
        run_max, run_total, accumulated = running
        block_length = key_block.shape[0]
        heads_of_keys = key_block.reshape(block_length, group_count, HEAD_SIZE)
        heads_of_values = value_block.reshape(block_length, slot_count, group_count, HEAD_SIZE)
        scores = (
            jnp.einsum(
                "rsgjd,kgd->sgjrk", grouped, heads_of_keys, preferred_element_type=jnp.float32
            )
            * inverse
        )
        visible = (block_positions[None, :] <= positions[:, None]) & (
            block_positions[None, :] < live_length
        )
        masked = jnp.where(visible, scores, -1e30)
        new_max = jnp.maximum(run_max, jnp.max(masked, axis=-1))
        weights = jnp.where(visible, jnp.exp(masked - new_max[..., None]), 0.0)
        factor = jnp.exp(run_max - new_max)
        new_total = run_total * factor + jnp.sum(weights, axis=-1)
        new_accumulated = accumulated * jnp.transpose(factor, (0, 3, 1, 2))[..., None] + jnp.einsum(
            "sgjrk,ksgd->srgjd",
            weights.astype(jnp.bfloat16),
            heads_of_values,
            preferred_element_type=jnp.float32,
        )
        return (new_max, new_total, new_accumulated)

    initial = (
        jnp.full((slot_count, group_count, group_portion, row_count), -1e30, jnp.float32),
        jnp.zeros((slot_count, group_count, group_portion, row_count), jnp.float32),
        jnp.zeros((slot_count, row_count, group_count, group_portion, HEAD_SIZE), jnp.float32),
    )
    piece_rows = keys.shape[0]
    step_rows = block_rows(piece_rows)

    def advance(block_index, current):
        offset = block_index * step_rows
        key_block = lax.dynamic_slice_in_dim(keys, offset, step_rows, 0)
        value_block = lax.dynamic_slice_in_dim(values, offset, step_rows, 0)
        block_positions = lax.dynamic_slice_in_dim(key_positions, offset, step_rows, 0)
        return update(current, key_block, value_block, block_positions)

    run_max, run_total, accumulated = lax.fori_loop(0, piece_rows // step_rows, advance, initial)
    result = accumulated / jnp.transpose(run_total, (0, 3, 1, 2))[..., None]
    return result.reshape(slot_count, row_count, group_count * group_portion * HEAD_SIZE).astype(
        jnp.bfloat16
    )


def per_device(
    activations,
    query_base,
    key_base,
    plain_value_rows,
    query_down,
    query_up,
    value_down,
    value_raise_factor,
    member_lists,
    prompt_lengths,
):
    row_count = activations.shape[1]
    member_ids = member_lists[0]
    slot_count = member_ids.shape[0]
    up_width = query_up.shape[2]
    group_count = key_base.shape[2] // HEAD_SIZE
    ctx = lax.axis_index("ctx")
    positions = ctx * row_count + jnp.arange(row_count, dtype=jnp.int32)
    downs = (query_down, value_down)
    ups = jnp.concatenate([query_up, value_raise_factor], axis=2)
    early = lax.axis_size("ctx") == 2
    if early:
        ups = ctx_gather(ups, 1, False)
    (down_half, up_half), first = select_members((downs, ups), member_ids, member_lists)
    ups = up_half if early else ctx_gather(up_half, 1, False)
    up_query = ups[..., :up_width]
    up_value = ups[..., up_width:]
    if lax.axis_size("ctx") == 2:
        local_rows, value_rows, keys, _ = lax.optimization_barrier(
            (activations[0], plain_value_rows[0], key_base[0], first)
        )
        tokens = ctx_gather(local_rows, 0, False)
        partial = jnp.stack(
            [jnp.einsum("rd,skd->rsk", tokens, h, preferred_element_type=jnp.float32) for h in down_half],
            axis=1,
        )
        mine = mp_sum(partial).astype(jnp.bfloat16)
        theirs = swap(mine, "ctx", 1)
        theirs = jnp.concatenate([theirs[row_count:], theirs[:row_count]], axis=0)
        ranks = jnp.concatenate([mine, theirs], axis=3)
        value_rows = ctx_gather(value_rows, 0, False)
        keys = ctx_gather(keys, 0, False)
        own_keys = jnp.arange(row_count, dtype=jnp.int32)
        key_positions = jnp.concatenate(
            [ctx * row_count + own_keys, (1 - ctx) * row_count + own_keys]
        )
        rank_query = ranks[:row_count, 0]
        rank_value = ranks[:, 1]
    else:
        partial = jnp.stack(
            [
                jnp.einsum(
                    "rd,skd->rsk",
                    activations[0],
                    ctx_gather(h, 1, False),
                    preferred_element_type=jnp.float32,
                )
                for h in down_half
            ],
            axis=1,
        )
        ranks = mp_sum(partial).astype(jnp.bfloat16)
        rank_query = ranks[:, 0]
        rank_value = ranks[:, 1]
        value_rows = plain_value_rows[0]
        keys = ctx_gather(key_base[0], 0, True)
        key_positions = jnp.arange(keys.shape[0], dtype=jnp.int32)
    query_matrix = (
        query_base[0][:, None, :]
        + jnp.einsum("rsk,skc->rsc", rank_query, up_query, preferred_element_type=jnp.float32)
    ).astype(jnp.bfloat16)
    group_portion = query_matrix.shape[2] // (group_count * HEAD_SIZE)
    grouped = query_matrix.reshape(row_count, slot_count, group_count, group_portion, HEAD_SIZE)
    built = (
        value_rows[:, None, :]
        + jnp.einsum("rsk,skc->rsc", rank_value, up_value, preferred_element_type=jnp.float32)
    ).astype(jnp.bfloat16)
    values = built.reshape(built.shape[0], slot_count * group_count * HEAD_SIZE)
    if lax.axis_size("ctx") != 2:
        values = ctx_gather(values, 0, True)
    result = attend(
        grouped, keys, values, key_positions, positions, prompt_lengths[0], slot_count
    )
    return result[:, None]


def solution(mesh):
    in_specs = (
        P("req", "ctx", "mp"),
        P("req", "ctx", "mp"),
        P("req", "ctx", "mp"),
        P("req", "ctx", "mp"),
        P("req", "ctx", "mp"),
        P("req", "ctx", "mp"),
        P("req", "ctx", "mp"),
        P("req", "ctx", "mp"),
        P("req", None),
        P("req"),
    )
    out_specs = P(None, "req", "ctx", "mp")
    return jax.shard_map(
        per_device, mesh=mesh, in_specs=in_specs, out_specs=out_specs, check_vma=False
    )
```

```python
import math

import jax
import jax.numpy as jnp
from jax import lax
from jax.sharding import PartitionSpec as P

HEAD_SIZE = 128


def block_rows(total_rows):
    if total_rows <= 512:
        return total_rows
    for candidate in range(512, 0, -1):
        if total_rows % candidate == 0:
            return candidate
    return total_rows


def swap(value, axis, bit):
    size = lax.axis_size(axis)
    return lax.ppermute(value, axis, [(i, i ^ bit) for i in range(size)])


def ctx_gather(mine, dim, ordered):
    if lax.axis_size("ctx") == 2:
        other = swap(mine, "ctx", 1)
        if not ordered:
            return jnp.concatenate([mine, other], axis=dim)
        first = lax.axis_index("ctx") == 0
        low = jnp.where(first, mine, other)
        high = jnp.where(first, other, mine)
        return jnp.concatenate([low, high], axis=dim)
    return lax.all_gather(mine, "ctx", axis=dim, tiled=True)


def mp_sum(value):
    size = lax.axis_size("mp")
    if size & (size - 1):
        return lax.psum(value, "mp")
    total = value
    for bit in range(1, size):
        total = total + swap(value, "mp", bit)
    return total


def select_members(factor_set, member_ids, member_lists, prepare=None):
    local_count = factor_set[0].shape[0]
    req_size = lax.axis_size("req")
    if req_size != 4:
        everything = [lax.all_gather(f, "req", axis=0, tiled=True) for f in factor_set]
        return [
            jnp.stack([lax.dynamic_index_in_dim(f, m, 0, keepdims=False) for m in member_ids])
            for f in everything
        ], everything[0]
    req = lax.axis_index("req")
    core = req % 2
    row = req // 2
    row_span = 2 * local_count
    far_ids = swap(member_lists, "req", 2)[0]

    def pick(own, partner, index):
        mine = lax.dynamic_index_in_dim(own, index % local_count, 0, keepdims=False)
        theirs = lax.dynamic_index_in_dim(partner, index % local_count, 0, keepdims=False)
        return jnp.where(index // local_count == core, mine, theirs)

    owns = []
    partners = []
    incoming = []
    previous = None
    for own in factor_set:
        if previous is not None:
            own = lax.optimization_barrier((own, previous[0]))[0]
            if prepare is not None:
                own = prepare(own)
        partner = swap(own, "req", 1)
        outgoing = jnp.stack(
            [pick(own, partner, far_ids[s] % row_span) for s in range(far_ids.shape[0])]
        )
        if previous is not None:
            outgoing = lax.optimization_barrier((outgoing, previous[1]))[0]
        received = swap(outgoing, "req", 2)
        owns.append(own)
        partners.append(partner)
        incoming.append(received)
        previous = (partner, received)
    chosen = []
    for own, partner, received in zip(owns, partners, incoming):
        slots = []
        for s in range(member_ids.shape[0]):
            m = member_ids[s]
            near = pick(own, partner, m % row_span)
            slots.append(jnp.where(m // row_span == row, near, received[s]))
        chosen.append(jnp.stack(slots))
    return chosen, partners[0]


def attend(grouped, keys, values, key_positions, positions, live_length, slot_count):
    row_count, _, group_count, group_portion, _ = grouped.shape
    inverse = 1.0 / math.sqrt(HEAD_SIZE)

    def update(running, key_block, value_block, block_positions):
        run_max, run_total, accumulated = running
        block_length = key_block.shape[0]
        heads_of_keys = key_block.reshape(block_length, group_count, HEAD_SIZE)
        heads_of_values = value_block.reshape(block_length, slot_count, group_count, HEAD_SIZE)
        scores = (
            jnp.einsum(
                "rsgjd,kgd->sgjrk", grouped, heads_of_keys, preferred_element_type=jnp.float32
            )
            * inverse
        )
        visible = (block_positions[None, :] <= positions[:, None]) & (
            block_positions[None, :] < live_length
        )
        masked = jnp.where(visible, scores, -1e30)
        new_max = jnp.maximum(run_max, jnp.max(masked, axis=-1))
        weights = jnp.where(visible, jnp.exp(masked - new_max[..., None]), 0.0)
        factor = jnp.exp(run_max - new_max)
        new_total = run_total * factor + jnp.sum(weights, axis=-1)
        new_accumulated = accumulated * factor[..., None] + jnp.einsum(
            "sgjrk,ksgd->sgjrd",
            weights.astype(jnp.bfloat16),
            heads_of_values,
            preferred_element_type=jnp.float32,
        )
        return (new_max, new_total, new_accumulated)

    initial = (
        jnp.full((slot_count, group_count, group_portion, row_count), -1e30, jnp.float32),
        jnp.zeros((slot_count, group_count, group_portion, row_count), jnp.float32),
        jnp.zeros((slot_count, group_count, group_portion, row_count, HEAD_SIZE), jnp.float32),
    )
    piece_rows = keys.shape[0]
    step_rows = block_rows(piece_rows)

    def advance(block_index, current):
        offset = block_index * step_rows
        key_block = lax.dynamic_slice_in_dim(keys, offset, step_rows, 0)
        value_block = lax.dynamic_slice_in_dim(values, offset, step_rows, 0)
        block_positions = lax.dynamic_slice_in_dim(key_positions, offset, step_rows, 0)
        return update(current, key_block, value_block, block_positions)

    run_max, run_total, accumulated = lax.fori_loop(0, piece_rows // step_rows, advance, initial)
    result = accumulated / run_total[..., None]
    return (
        jnp.transpose(result, (0, 3, 1, 2, 4))
        .reshape(slot_count, row_count, group_count * group_portion * HEAD_SIZE)
        .astype(jnp.bfloat16)
    )


def per_device(
    activations,
    query_base,
    key_base,
    plain_value_rows,
    query_down,
    query_up,
    value_down,
    value_raise_factor,
    member_lists,
    prompt_lengths,
):
    row_count = activations.shape[1]
    member_ids = member_lists[0]
    slot_count = member_ids.shape[0]
    up_width = query_up.shape[2]
    group_count = key_base.shape[2] // HEAD_SIZE
    ctx = lax.axis_index("ctx")
    positions = ctx * row_count + jnp.arange(row_count, dtype=jnp.int32)
    downs = jnp.stack([query_down, value_down], axis=1)
    ups = jnp.concatenate([query_up, value_raise_factor], axis=2)
    early = lax.axis_size("ctx") == 2 and lax.axis_size("req") == 4
    prepare = (lambda value: ctx_gather(value, 1, False)) if early else None
    (down_half, up_half), first = select_members(
        (downs, ups), member_ids, member_lists, prepare
    )
    ups = up_half if early else ctx_gather(up_half, 1, False)
    up_query = ups[..., :up_width]
    up_value = ups[..., up_width:]
    if lax.axis_size("ctx") == 2:
        local_rows, value_rows, keys, _ = lax.optimization_barrier(
            (activations[0], plain_value_rows[0], key_base[0], first)
        )
        tokens = ctx_gather(local_rows, 0, False)
        partial = jnp.einsum("rd,sfkd->rfsk", tokens, down_half, preferred_element_type=jnp.float32)
        mine = mp_sum(partial).astype(jnp.bfloat16)
        theirs = swap(mine, "ctx", 1)
        theirs = jnp.concatenate([theirs[row_count:], theirs[:row_count]], axis=0)
        ranks = jnp.concatenate([mine, theirs], axis=3)
        value_rows = ctx_gather(value_rows, 0, False)
        keys = ctx_gather(keys, 0, False)
        own_keys = jnp.arange(row_count, dtype=jnp.int32)
        key_positions = jnp.concatenate(
            [ctx * row_count + own_keys, (1 - ctx) * row_count + own_keys]
        )
        rank_query = ranks[:row_count, 0]
        rank_value = ranks[:, 1]
    else:
        downs = ctx_gather(down_half, 2, False)
        partial = jnp.einsum(
            "rd,sfkd->rfsk", activations[0], downs, preferred_element_type=jnp.float32
        )
        ranks = mp_sum(partial).astype(jnp.bfloat16)
        rank_query = ranks[:, 0]
        rank_value = ranks[:, 1]
        value_rows = plain_value_rows[0]
        keys = ctx_gather(key_base[0], 0, True)
        key_positions = jnp.arange(keys.shape[0], dtype=jnp.int32)
    query_matrix = (
        query_base[0][:, None, :]
        + jnp.einsum("rsk,skc->rsc", rank_query, up_query, preferred_element_type=jnp.float32)
    ).astype(jnp.bfloat16)
    group_portion = query_matrix.shape[2] // (group_count * HEAD_SIZE)
    grouped = query_matrix.reshape(row_count, slot_count, group_count, group_portion, HEAD_SIZE)
    built = (
        value_rows[:, None, :]
        + jnp.einsum("rsk,skc->rsc", rank_value, up_value, preferred_element_type=jnp.float32)
    ).astype(jnp.bfloat16)
    values = built.reshape(built.shape[0], slot_count * group_count * HEAD_SIZE)
    if lax.axis_size("ctx") != 2:
        values = ctx_gather(values, 0, True)
    result = attend(
        grouped, keys, values, key_positions, positions, prompt_lengths[0], slot_count
    )
    return result[:, None]


def solution(mesh):
    in_specs = (
        P("req", "ctx", "mp"),
        P("req", "ctx", "mp"),
        P("req", "ctx", "mp"),
        P("req", "ctx", "mp"),
        P("req", "ctx", "mp"),
        P("req", "ctx", "mp"),
        P("req", "ctx", "mp"),
        P("req", "ctx", "mp"),
        P("req", None),
        P("req"),
    )
    out_specs = P(None, "req", "ctx", "mp")
    return jax.shard_map(
        per_device, mesh=mesh, in_specs=in_specs, out_specs=out_specs, check_vma=False
    )
```

```python
import math

import jax
import jax.numpy as jnp
from jax import lax
from jax.sharding import PartitionSpec as P

HEAD_SIZE = 128


def block_rows(total_rows):
    if total_rows <= 512:
        return total_rows
    for candidate in range(512, 0, -1):
        if total_rows % candidate == 0:
            return candidate
    return total_rows


def swap(value, axis, bit):
    size = lax.axis_size(axis)
    return lax.ppermute(value, axis, [(i, i ^ bit) for i in range(size)])


def ctx_gather(mine, dim, ordered):
    if lax.axis_size("ctx") == 2:
        other = swap(mine, "ctx", 1)
        if not ordered:
            return jnp.concatenate([mine, other], axis=dim)
        first = lax.axis_index("ctx") == 0
        low = jnp.where(first, mine, other)
        high = jnp.where(first, other, mine)
        return jnp.concatenate([low, high], axis=dim)
    return lax.all_gather(mine, "ctx", axis=dim, tiled=True)


def mp_sum(value):
    size = lax.axis_size("mp")
    if size & (size - 1):
        return lax.psum(value, "mp")
    total = value
    for bit in range(1, size):
        total = total + swap(value, "mp", bit)
    return total


def select_members(factor_set, member_ids, member_lists, prepare=None):
    local_count = factor_set[0].shape[0]
    req_size = lax.axis_size("req")
    if req_size != 4:
        everything = [lax.all_gather(f, "req", axis=0, tiled=True) for f in factor_set]
        return [
            jnp.stack([lax.dynamic_index_in_dim(f, m, 0, keepdims=False) for m in member_ids])
            for f in everything
        ], everything[0]
    req = lax.axis_index("req")
    core = req % 2
    row = req // 2
    row_span = 2 * local_count
    far_ids = swap(member_lists, "req", 2)[0]

    def pick(own, partner, index):
        mine = lax.dynamic_index_in_dim(own, index % local_count, 0, keepdims=False)
        theirs = lax.dynamic_index_in_dim(partner, index % local_count, 0, keepdims=False)
        return jnp.where(index // local_count == core, mine, theirs)

    owns = []
    partners = []
    incoming = []
    previous = None
    for own in factor_set:
        if previous is not None:
            own = lax.optimization_barrier((own, previous[0]))[0]
            if prepare is not None:
                own = prepare(own)
        partner = swap(own, "req", 1)
        outgoing = jnp.stack(
            [pick(own, partner, far_ids[s] % row_span) for s in range(far_ids.shape[0])]
        )
        if previous is not None:
            outgoing = lax.optimization_barrier((outgoing, previous[1]))[0]
        received = swap(outgoing, "req", 2)
        owns.append(own)
        partners.append(partner)
        incoming.append(received)
        previous = (partner, received)
    chosen = []
    for own, partner, received in zip(owns, partners, incoming):
        slots = []
        for s in range(member_ids.shape[0]):
            m = member_ids[s]
            near = pick(own, partner, m % row_span)
            slots.append(jnp.where(m // row_span == row, near, received[s]))
        chosen.append(jnp.stack(slots))
    return chosen, partners[0]


def attend(grouped, keys, values, key_positions, positions, live_length, slot_count):
    row_count, _, group_count, group_portion, _ = grouped.shape
    inverse = 1.0 / math.sqrt(HEAD_SIZE)

    def update(running, key_block, value_block, block_positions):
        run_max, run_total, accumulated = running
        block_length = key_block.shape[0]
        heads_of_keys = key_block.reshape(block_length, group_count, HEAD_SIZE)
        heads_of_values = value_block.reshape(block_length, slot_count, group_count, HEAD_SIZE)
        scores = (
            jnp.einsum(
                "rsgjd,kgd->sgjrk", grouped, heads_of_keys, preferred_element_type=jnp.float32
            )
            * inverse
        )
        visible = (block_positions[None, :] <= positions[:, None]) & (
            block_positions[None, :] < live_length
        )
        masked = jnp.where(visible, scores, -1e30)
        new_max = jnp.maximum(run_max, jnp.max(masked, axis=-1))
        weights = jnp.where(visible, jnp.exp(masked - new_max[..., None]), 0.0)
        factor = jnp.exp(run_max - new_max)
        new_total = run_total * factor + jnp.sum(weights, axis=-1)
        new_accumulated = accumulated * factor[..., None] + jnp.einsum(
            "sgjrk,ksgd->sgjrd",
            weights.astype(jnp.bfloat16),
            heads_of_values,
            preferred_element_type=jnp.float32,
        )
        return (new_max, new_total, new_accumulated)

    initial = (
        jnp.full((slot_count, group_count, group_portion, row_count), -1e30, jnp.float32),
        jnp.zeros((slot_count, group_count, group_portion, row_count), jnp.float32),
        jnp.zeros((slot_count, group_count, group_portion, row_count, HEAD_SIZE), jnp.float32),
    )
    piece_rows = keys.shape[0]
    step_rows = block_rows(piece_rows)

    def advance(block_index, current):
        offset = block_index * step_rows
        key_block = lax.dynamic_slice_in_dim(keys, offset, step_rows, 0)
        value_block = lax.dynamic_slice_in_dim(values, offset, step_rows, 0)
        block_positions = lax.dynamic_slice_in_dim(key_positions, offset, step_rows, 0)
        return update(current, key_block, value_block, block_positions)

    run_max, run_total, accumulated = lax.fori_loop(0, piece_rows // step_rows, advance, initial)
    result = accumulated / run_total[..., None]
    return (
        jnp.transpose(result, (0, 3, 1, 2, 4))
        .reshape(slot_count, row_count, group_count * group_portion * HEAD_SIZE)
        .astype(jnp.bfloat16)
    )


def per_device(
    activations,
    query_base,
    key_base,
    plain_value_rows,
    query_down,
    query_up,
    value_down,
    value_raise_factor,
    member_lists,
    prompt_lengths,
):
    row_count = activations.shape[1]
    member_ids = member_lists[0]
    slot_count = member_ids.shape[0]
    up_width = query_up.shape[2]
    group_count = key_base.shape[2] // HEAD_SIZE
    ctx = lax.axis_index("ctx")
    positions = ctx * row_count + jnp.arange(row_count, dtype=jnp.int32)
    downs = jnp.stack([query_down, value_down], axis=1)
    ups = jnp.concatenate([query_up, value_raise_factor], axis=2)
    early = lax.axis_size("ctx") == 2 and lax.axis_size("req") == 4
    prepare = None
    if lax.axis_size("ctx") == 2:
        tokens = ctx_gather(activations[0], 0, False)
    if early:
        def prepare(value):
            return ctx_gather(lax.optimization_barrier((value, tokens))[0], 1, False)

    (down_half, up_half), first = select_members(
        (downs, ups), member_ids, member_lists, prepare
    )
    ups = up_half if early else ctx_gather(up_half, 1, False)
    up_query = ups[..., :up_width]
    up_value = ups[..., up_width:]
    if lax.axis_size("ctx") == 2:
        value_rows, keys = plain_value_rows[0], key_base[0]
        partial = jnp.einsum("rd,sfkd->rfsk", tokens, down_half, preferred_element_type=jnp.float32)
        mine = mp_sum(partial).astype(jnp.bfloat16)
        theirs = swap(mine, "ctx", 1)
        theirs = jnp.concatenate([theirs[row_count:], theirs[:row_count]], axis=0)
        ranks = jnp.concatenate([mine, theirs], axis=3)
        value_rows = ctx_gather(value_rows, 0, False)
        keys = ctx_gather(keys, 0, False)
        own_keys = jnp.arange(row_count, dtype=jnp.int32)
        key_positions = jnp.concatenate(
            [ctx * row_count + own_keys, (1 - ctx) * row_count + own_keys]
        )
        rank_query = ranks[:row_count, 0]
        rank_value = ranks[:, 1]
    else:
        downs = ctx_gather(down_half, 2, False)
        partial = jnp.einsum(
            "rd,sfkd->rfsk", activations[0], downs, preferred_element_type=jnp.float32
        )
        ranks = mp_sum(partial).astype(jnp.bfloat16)
        rank_query = ranks[:, 0]
        rank_value = ranks[:, 1]
        value_rows = plain_value_rows[0]
        keys = ctx_gather(key_base[0], 0, True)
        key_positions = jnp.arange(keys.shape[0], dtype=jnp.int32)
    query_matrix = (
        query_base[0][:, None, :]
        + jnp.einsum("rsk,skc->rsc", rank_query, up_query, preferred_element_type=jnp.float32)
    ).astype(jnp.bfloat16)
    group_portion = query_matrix.shape[2] // (group_count * HEAD_SIZE)
    grouped = query_matrix.reshape(row_count, slot_count, group_count, group_portion, HEAD_SIZE)
    built = (
        value_rows[:, None, :]
        + jnp.einsum("rsk,skc->rsc", rank_value, up_value, preferred_element_type=jnp.float32)
    ).astype(jnp.bfloat16)
    values = built.reshape(built.shape[0], slot_count * group_count * HEAD_SIZE)
    if lax.axis_size("ctx") != 2:
        values = ctx_gather(values, 0, True)
    result = attend(
        grouped, keys, values, key_positions, positions, prompt_lengths[0], slot_count
    )
    return result[:, None]


def solution(mesh):
    in_specs = (
        P("req", "ctx", "mp"),
        P("req", "ctx", "mp"),
        P("req", "ctx", "mp"),
        P("req", "ctx", "mp"),
        P("req", "ctx", "mp"),
        P("req", "ctx", "mp"),
        P("req", "ctx", "mp"),
        P("req", "ctx", "mp"),
        P("req", None),
        P("req"),
    )
    out_specs = P(None, "req", "ctx", "mp")
    return jax.shard_map(
        per_device, mesh=mesh, in_specs=in_specs, out_specs=out_specs, check_vma=False
    )
```

```python
import math

import jax
import jax.numpy as jnp
from jax import lax
from jax.sharding import PartitionSpec as P

HEAD_SIZE = 128


def block_rows(total_rows):
    if total_rows <= 512:
        return total_rows
    for candidate in range(512, 0, -1):
        if total_rows % candidate == 0:
            return candidate
    return total_rows


def swap(value, axis, bit):
    size = lax.axis_size(axis)
    return lax.ppermute(value, axis, [(i, i ^ bit) for i in range(size)])


def ctx_gather(mine, dim, ordered):
    if lax.axis_size("ctx") == 2:
        other = swap(mine, "ctx", 1)
        if not ordered:
            return jnp.concatenate([mine, other], axis=dim)
        first = lax.axis_index("ctx") == 0
        low = jnp.where(first, mine, other)
        high = jnp.where(first, other, mine)
        return jnp.concatenate([low, high], axis=dim)
    return lax.all_gather(mine, "ctx", axis=dim, tiled=True)


def mp_sum(value):
    size = lax.axis_size("mp")
    if size & (size - 1):
        return lax.psum(value, "mp")
    bit = 1
    while bit < size:
        value = value + swap(value, "mp", bit)
        bit *= 2
    return value


def select_members(factor_set, member_ids, member_lists, prepare=None):
    local_count = factor_set[0].shape[0]
    req_size = lax.axis_size("req")
    if req_size != 4:
        everything = [lax.all_gather(f, "req", axis=0, tiled=True) for f in factor_set]
        return [
            jnp.stack([lax.dynamic_index_in_dim(f, m, 0, keepdims=False) for m in member_ids])
            for f in everything
        ], everything[0]
    req = lax.axis_index("req")
    core = req % 2
    row = req // 2
    row_span = 2 * local_count
    far_ids = swap(member_lists, "req", 2)[0]

    def pick(own, partner, index):
        mine = lax.dynamic_index_in_dim(own, index % local_count, 0, keepdims=False)
        theirs = lax.dynamic_index_in_dim(partner, index % local_count, 0, keepdims=False)
        return jnp.where(index // local_count == core, mine, theirs)

    owns = []
    partners = []
    incoming = []
    previous = None
    for own in factor_set:
        if previous is not None:
            own = lax.optimization_barrier((own, previous[0]))[0]
            if prepare is not None:
                own = prepare(own)
        partner = swap(own, "req", 1)
        outgoing = jnp.stack(
            [pick(own, partner, far_ids[s] % row_span) for s in range(far_ids.shape[0])]
        )
        if previous is not None:
            outgoing = lax.optimization_barrier((outgoing, previous[1]))[0]
        received = swap(outgoing, "req", 2)
        owns.append(own)
        partners.append(partner)
        incoming.append(received)
        previous = (partner, received)
    chosen = []
    for own, partner, received in zip(owns, partners, incoming):
        slots = []
        for s in range(member_ids.shape[0]):
            m = member_ids[s]
            near = pick(own, partner, m % row_span)
            slots.append(jnp.where(m // row_span == row, near, received[s]))
        chosen.append(jnp.stack(slots))
    return chosen, partners[0]


def attend(grouped, keys, values, key_positions, positions, live_length, slot_count):
    row_count, _, group_count, group_portion, _ = grouped.shape
    inverse = 1.0 / math.sqrt(HEAD_SIZE)

    def update(running, key_block, value_block, block_positions):
        run_max, run_total, accumulated = running
        block_length = key_block.shape[0]
        heads_of_keys = key_block.reshape(block_length, group_count, HEAD_SIZE)
        heads_of_values = value_block.reshape(block_length, slot_count, group_count, HEAD_SIZE)
        scores = (
            jnp.einsum(
                "rsgjd,kgd->sgjrk", grouped, heads_of_keys, preferred_element_type=jnp.float32
            )
            * inverse
        )
        visible = (block_positions[None, :] <= positions[:, None]) & (
            block_positions[None, :] < live_length
        )
        masked = jnp.where(visible, scores, -1e30)
        new_max = jnp.maximum(run_max, jnp.max(masked, axis=-1))
        weights = jnp.where(visible, jnp.exp(masked - new_max[..., None]), 0.0)
        factor = jnp.exp(run_max - new_max)
        new_total = run_total * factor + jnp.sum(weights, axis=-1)
        new_accumulated = accumulated * factor[..., None] + jnp.einsum(
            "sgjrk,ksgd->sgjrd",
            weights.astype(jnp.bfloat16),
            heads_of_values,
            preferred_element_type=jnp.float32,
        )
        return (new_max, new_total, new_accumulated)

    initial = (
        jnp.full((slot_count, group_count, group_portion, row_count), -1e30, jnp.float32),
        jnp.zeros((slot_count, group_count, group_portion, row_count), jnp.float32),
        jnp.zeros((slot_count, group_count, group_portion, row_count, HEAD_SIZE), jnp.float32),
    )
    piece_rows = keys.shape[0]
    step_rows = block_rows(piece_rows)

    def advance(block_index, current):
        offset = block_index * step_rows
        key_block = lax.dynamic_slice_in_dim(keys, offset, step_rows, 0)
        value_block = lax.dynamic_slice_in_dim(values, offset, step_rows, 0)
        block_positions = lax.dynamic_slice_in_dim(key_positions, offset, step_rows, 0)
        return update(current, key_block, value_block, block_positions)

    run_max, run_total, accumulated = lax.fori_loop(0, piece_rows // step_rows, advance, initial)
    result = accumulated / run_total[..., None]
    return (
        jnp.transpose(result, (0, 3, 1, 2, 4))
        .reshape(slot_count, row_count, group_count * group_portion * HEAD_SIZE)
        .astype(jnp.bfloat16)
    )


def per_device(
    activations,
    query_base,
    key_base,
    plain_value_rows,
    query_down,
    query_up,
    value_down,
    value_raise_factor,
    member_lists,
    prompt_lengths,
):
    row_count = activations.shape[1]
    member_ids = member_lists[0]
    slot_count = member_ids.shape[0]
    up_width = query_up.shape[2]
    group_count = key_base.shape[2] // HEAD_SIZE
    ctx = lax.axis_index("ctx")
    positions = ctx * row_count + jnp.arange(row_count, dtype=jnp.int32)
    downs = jnp.stack([query_down, value_down], axis=1)
    ups = jnp.concatenate([query_up, value_raise_factor], axis=2)
    early = lax.axis_size("ctx") == 2 and lax.axis_size("req") == 4
    prepare = (lambda value: ctx_gather(value, 1, False)) if early else None
    (down_half, up_half), first = select_members(
        (downs, ups), member_ids, member_lists, prepare
    )
    ups = up_half if early else ctx_gather(up_half, 1, False)
    up_query = ups[..., :up_width]
    up_value = ups[..., up_width:]
    if lax.axis_size("ctx") == 2:
        local_rows, value_rows, keys, _ = lax.optimization_barrier(
            (activations[0], plain_value_rows[0], key_base[0], first)
        )
        tokens = ctx_gather(local_rows, 0, False)
        partial = jnp.einsum("rd,sfkd->rfsk", tokens, down_half, preferred_element_type=jnp.float32)
        mine = mp_sum(partial).astype(jnp.bfloat16)
        theirs = swap(mine, "ctx", 1)
        theirs = jnp.concatenate([theirs[row_count:], theirs[:row_count]], axis=0)
        ranks = jnp.concatenate([mine, theirs], axis=3)
        value_rows = ctx_gather(value_rows, 0, False)
        keys = ctx_gather(keys, 0, False)
        own_keys = jnp.arange(row_count, dtype=jnp.int32)
        key_positions = jnp.concatenate(
            [ctx * row_count + own_keys, (1 - ctx) * row_count + own_keys]
        )
        rank_query = ranks[:row_count, 0]
        rank_value = ranks[:, 1]
    else:
        downs = ctx_gather(down_half, 2, False)
        partial = jnp.einsum(
            "rd,sfkd->rfsk", activations[0], downs, preferred_element_type=jnp.float32
        )
        ranks = mp_sum(partial).astype(jnp.bfloat16)
        rank_query = ranks[:, 0]
        rank_value = ranks[:, 1]
        value_rows = plain_value_rows[0]
        keys = ctx_gather(key_base[0], 0, True)
        key_positions = jnp.arange(keys.shape[0], dtype=jnp.int32)
    query_matrix = (
        query_base[0][:, None, :]
        + jnp.einsum("rsk,skc->rsc", rank_query, up_query, preferred_element_type=jnp.float32)
    ).astype(jnp.bfloat16)
    group_portion = query_matrix.shape[2] // (group_count * HEAD_SIZE)
    grouped = query_matrix.reshape(row_count, slot_count, group_count, group_portion, HEAD_SIZE)
    built = (
        value_rows[:, None, :]
        + jnp.einsum("rsk,skc->rsc", rank_value, up_value, preferred_element_type=jnp.float32)
    ).astype(jnp.bfloat16)
    values = built.reshape(built.shape[0], slot_count * group_count * HEAD_SIZE)
    if lax.axis_size("ctx") != 2:
        values = ctx_gather(values, 0, True)
    result = attend(
        grouped, keys, values, key_positions, positions, prompt_lengths[0], slot_count
    )
    return result[:, None]


def solution(mesh):
    in_specs = (
        P("req", "ctx", "mp"),
        P("req", "ctx", "mp"),
        P("req", "ctx", "mp"),
        P("req", "ctx", "mp"),
        P("req", "ctx", "mp"),
        P("req", "ctx", "mp"),
        P("req", "ctx", "mp"),
        P("req", "ctx", "mp"),
        P("req", None),
        P("req"),
    )
    out_specs = P(None, "req", "ctx", "mp")
    return jax.shard_map(
        per_device, mesh=mesh, in_specs=in_specs, out_specs=out_specs, check_vma=False
    )
```

```python
import math

import jax
import jax.numpy as jnp
from jax import lax
from jax.sharding import PartitionSpec as P

HEAD_SIZE = 128


def block_rows(total_rows):
    if total_rows <= 512:
        return total_rows
    for candidate in range(512, 0, -1):
        if total_rows % candidate == 0:
            return candidate
    return total_rows


def swap(value, axis, bit):
    size = lax.axis_size(axis)
    return lax.ppermute(value, axis, [(i, i ^ bit) for i in range(size)])


def ctx_gather(mine, dim, ordered):
    if lax.axis_size("ctx") == 2:
        other = swap(mine, "ctx", 1)
        if not ordered:
            return jnp.concatenate([mine, other], axis=dim)
        first = lax.axis_index("ctx") == 0
        low = jnp.where(first, mine, other)
        high = jnp.where(first, other, mine)
        return jnp.concatenate([low, high], axis=dim)
    return lax.all_gather(mine, "ctx", axis=dim, tiled=True)


def mp_sum(value):
    size = lax.axis_size("mp")
    if size & (size - 1):
        return lax.psum(value, "mp")
    total = value
    for bit in range(1, size):
        total = total + swap(value, "mp", bit)
    return total


def select_members(factor_set, member_ids, member_lists, prepare=None):
    local_count = factor_set[0].shape[0]
    req_size = lax.axis_size("req")
    if req_size != 4:
        everything = [lax.all_gather(f, "req", axis=0, tiled=True) for f in factor_set]
        return [
            jnp.stack([lax.dynamic_index_in_dim(f, m, 0, keepdims=False) for m in member_ids])
            for f in everything
        ], everything[0]
    req = lax.axis_index("req")
    core = req % 2
    row = req // 2
    row_span = 2 * local_count
    far_ids = swap(member_lists, "req", 2)[0]

    def pick(own, partner, index):
        mine = lax.dynamic_index_in_dim(own, index % local_count, 0, keepdims=False)
        theirs = lax.dynamic_index_in_dim(partner, index % local_count, 0, keepdims=False)
        return jnp.where(index // local_count == core, mine, theirs)

    owns = []
    partners = []
    incoming = []
    previous = None
    for own in factor_set:
        if previous is not None:
            own = lax.optimization_barrier((own, previous[0]))[0]
            if prepare is not None:
                own = prepare(own)
        partner = swap(own, "req", 1)
        outgoing = jnp.stack(
            [pick(own, partner, far_ids[s] % row_span) for s in range(far_ids.shape[0])]
        )
        if previous is not None:
            outgoing = lax.optimization_barrier((outgoing, previous[1]))[0]
        received = swap(outgoing, "req", 2)
        owns.append(own)
        partners.append(partner)
        incoming.append(received)
        previous = (partner, received)
    chosen = []
    for own, partner, received in zip(owns, partners, incoming):
        slots = []
        for s in range(member_ids.shape[0]):
            m = member_ids[s]
            near = pick(own, partner, m % row_span)
            slots.append(jnp.where(m // row_span == row, near, received[s]))
        chosen.append(jnp.stack(slots))
    return chosen, partners[0]


def attend(grouped, keys, values, key_positions, positions, live_length, slot_count):
    row_count, _, group_count, group_portion, _ = grouped.shape
    inverse = 1.0 / math.sqrt(HEAD_SIZE)

    def update(running, key_block, value_block, block_positions):
        run_max, run_total, accumulated = running
        block_length = key_block.shape[0]
        heads_of_keys = key_block.reshape(block_length, group_count, HEAD_SIZE)
        heads_of_values = value_block.reshape(block_length, slot_count, group_count, HEAD_SIZE)
        scores = (
            jnp.einsum(
                "rsgjd,kgd->sgjrk", grouped, heads_of_keys, preferred_element_type=jnp.float32
            )
            * inverse
        )
        visible = (block_positions[None, :] <= positions[:, None]) & (
            block_positions[None, :] < live_length
        )
        masked = jnp.where(visible, scores, -1e30)
        new_max = jnp.maximum(run_max, jnp.max(masked, axis=-1))
        weights = jnp.where(visible, jnp.exp(masked - new_max[..., None]), 0.0)
        factor = jnp.exp(run_max - new_max)
        new_total = run_total * factor + jnp.sum(weights, axis=-1)
        new_accumulated = accumulated * factor[..., None] + jnp.einsum(
            "sgjrk,ksgd->sgjrd",
            weights.astype(jnp.bfloat16),
            heads_of_values,
            preferred_element_type=jnp.float32,
        )
        return (new_max, new_total, new_accumulated)

    initial = (
        jnp.full((slot_count, group_count, group_portion, row_count), -1e30, jnp.float32),
        jnp.zeros((slot_count, group_count, group_portion, row_count), jnp.float32),
        jnp.zeros((slot_count, group_count, group_portion, row_count, HEAD_SIZE), jnp.float32),
    )
    piece_rows = keys.shape[0]
    step_rows = block_rows(piece_rows)

    def advance(block_index, current):
        offset = block_index * step_rows
        key_block = lax.dynamic_slice_in_dim(keys, offset, step_rows, 0)
        value_block = lax.dynamic_slice_in_dim(values, offset, step_rows, 0)
        block_positions = lax.dynamic_slice_in_dim(key_positions, offset, step_rows, 0)
        return update(current, key_block, value_block, block_positions)

    run_max, run_total, accumulated = lax.fori_loop(0, piece_rows // step_rows, advance, initial)
    result = accumulated / run_total[..., None]
    return (
        jnp.transpose(result, (0, 3, 1, 2, 4))
        .reshape(slot_count, row_count, group_count * group_portion * HEAD_SIZE)
        .astype(jnp.bfloat16)
    )


def per_device(
    activations,
    query_base,
    key_base,
    plain_value_rows,
    query_down,
    query_up,
    value_down,
    value_raise_factor,
    member_lists,
    prompt_lengths,
):
    row_count = activations.shape[1]
    member_ids = member_lists[0]
    slot_count = member_ids.shape[0]
    up_width = query_up.shape[2]
    group_count = key_base.shape[2] // HEAD_SIZE
    ctx = lax.axis_index("ctx")
    positions = ctx * row_count + jnp.arange(row_count, dtype=jnp.int32)
    downs = jnp.stack([query_down, value_down], axis=1)
    ups = jnp.concatenate([query_up, value_raise_factor], axis=2)
    early = lax.axis_size("ctx") == 2 and lax.axis_size("req") == 4
    prepare = None
    carried = {}
    if early:
        def prepare(value):
            local_rows = activations[0]
            flat = value.reshape(-1, local_rows.shape[1])
            other = swap(jnp.concatenate([local_rows, flat], axis=0), "ctx", 1)
            carried["tokens"] = jnp.concatenate([local_rows, other[:row_count]], axis=0)
            far = other[row_count:].reshape(value.shape)
            return jnp.concatenate([value, far], axis=1)

    (down_half, up_half), first = select_members(
        (downs, ups), member_ids, member_lists, prepare
    )
    ups = up_half if early else ctx_gather(up_half, 1, False)
    up_query = ups[..., :up_width]
    up_value = ups[..., up_width:]
    if lax.axis_size("ctx") == 2:
        if "tokens" in carried:
            tokens = carried["tokens"]
            value_rows, keys, _ = lax.optimization_barrier(
                (plain_value_rows[0], key_base[0], first)
            )
        else:
            local_rows, value_rows, keys, _ = lax.optimization_barrier(
                (activations[0], plain_value_rows[0], key_base[0], first)
            )
            tokens = ctx_gather(local_rows, 0, False)
        key_width = keys.shape[1]
        both = ctx_gather(jnp.concatenate([keys, value_rows], axis=1), 0, False)
        keys = both[:, :key_width]
        value_rows = both[:, key_width:]
        partial = jnp.einsum("rd,sfkd->rfsk", tokens, down_half, preferred_element_type=jnp.float32)
        mine = mp_sum(partial).astype(jnp.bfloat16)
        theirs = swap(mine, "ctx", 1)
        theirs = jnp.concatenate([theirs[row_count:], theirs[:row_count]], axis=0)
        ranks = jnp.concatenate([mine, theirs], axis=3)
        own_keys = jnp.arange(row_count, dtype=jnp.int32)
        key_positions = jnp.concatenate(
            [ctx * row_count + own_keys, (1 - ctx) * row_count + own_keys]
        )
        rank_query = ranks[:row_count, 0]
        rank_value = ranks[:, 1]
    else:
        downs = ctx_gather(down_half, 2, False)
        partial = jnp.einsum(
            "rd,sfkd->rfsk", activations[0], downs, preferred_element_type=jnp.float32
        )
        ranks = mp_sum(partial).astype(jnp.bfloat16)
        rank_query = ranks[:, 0]
        rank_value = ranks[:, 1]
        value_rows = plain_value_rows[0]
        keys = ctx_gather(key_base[0], 0, True)
        key_positions = jnp.arange(keys.shape[0], dtype=jnp.int32)
    query_matrix = (
        query_base[0][:, None, :]
        + jnp.einsum("rsk,skc->rsc", rank_query, up_query, preferred_element_type=jnp.float32)
    ).astype(jnp.bfloat16)
    group_portion = query_matrix.shape[2] // (group_count * HEAD_SIZE)
    grouped = query_matrix.reshape(row_count, slot_count, group_count, group_portion, HEAD_SIZE)
    built = (
        value_rows[:, None, :]
        + jnp.einsum("rsk,skc->rsc", rank_value, up_value, preferred_element_type=jnp.float32)
    ).astype(jnp.bfloat16)
    values = built.reshape(built.shape[0], slot_count * group_count * HEAD_SIZE)
    if lax.axis_size("ctx") != 2:
        values = ctx_gather(values, 0, True)
    result = attend(
        grouped, keys, values, key_positions, positions, prompt_lengths[0], slot_count
    )
    return result[:, None]


def solution(mesh):
    in_specs = (
        P("req", "ctx", "mp"),
        P("req", "ctx", "mp"),
        P("req", "ctx", "mp"),
        P("req", "ctx", "mp"),
        P("req", "ctx", "mp"),
        P("req", "ctx", "mp"),
        P("req", "ctx", "mp"),
        P("req", "ctx", "mp"),
        P("req", None),
        P("req"),
    )
    out_specs = P(None, "req", "ctx", "mp")
    return jax.shard_map(
        per_device, mesh=mesh, in_specs=in_specs, out_specs=out_specs, check_vma=False
    )
```

```python
import math

import jax
import jax.numpy as jnp
from jax import lax
from jax.sharding import PartitionSpec as P

HEAD_SIZE = 128


def block_rows(total_rows):
    if total_rows <= 512:
        return total_rows
    for candidate in range(512, 0, -1):
        if total_rows % candidate == 0:
            return candidate
    return total_rows


def swap(value, axis, bit):
    size = lax.axis_size(axis)
    return lax.ppermute(value, axis, [(i, i ^ bit) for i in range(size)])


def ctx_gather(mine, dim, ordered):
    if lax.axis_size("ctx") == 2:
        other = swap(mine, "ctx", 1)
        if not ordered:
            return jnp.concatenate([mine, other], axis=dim)
        first = lax.axis_index("ctx") == 0
        low = jnp.where(first, mine, other)
        high = jnp.where(first, other, mine)
        return jnp.concatenate([low, high], axis=dim)
    return lax.all_gather(mine, "ctx", axis=dim, tiled=True)


def mp_sum(value):
    size = lax.axis_size("mp")
    if size & (size - 1):
        return lax.psum(value, "mp")
    total = value
    for bit in range(1, size):
        total = total + swap(value, "mp", bit)
    return total


def select_members(factor_set, member_ids, member_lists, prepare=None):
    local_count = factor_set[0].shape[0]
    req_size = lax.axis_size("req")
    if req_size != 4:
        everything = [lax.all_gather(f, "req", axis=0, tiled=True) for f in factor_set]
        return [
            jnp.stack([lax.dynamic_index_in_dim(f, m, 0, keepdims=False) for m in member_ids])
            for f in everything
        ], everything[0]
    req = lax.axis_index("req")
    core = req % 2
    row = req // 2
    row_span = 2 * local_count
    far_ids = swap(member_lists, "req", 2)[0]

    def pick(own, partner, index):
        mine = lax.dynamic_index_in_dim(own, index % local_count, 0, keepdims=False)
        theirs = lax.dynamic_index_in_dim(partner, index % local_count, 0, keepdims=False)
        return jnp.where(index // local_count == core, mine, theirs)

    owns = []
    partners = []
    incoming = []
    previous = None
    for own in factor_set:
        if previous is not None:
            own = lax.optimization_barrier((own, previous[0]))[0]
            if prepare is not None:
                own = prepare(own)
        partner = swap(own, "req", 1)
        outgoing = jnp.stack(
            [pick(own, partner, far_ids[s] % row_span) for s in range(far_ids.shape[0])]
        )
        if previous is not None:
            outgoing = lax.optimization_barrier((outgoing, previous[1]))[0]
        received = swap(outgoing, "req", 2)
        owns.append(own)
        partners.append(partner)
        incoming.append(received)
        previous = (partner, received)
    chosen = []
    for own, partner, received in zip(owns, partners, incoming):
        slots = []
        for s in range(member_ids.shape[0]):
            m = member_ids[s]
            near = pick(own, partner, m % row_span)
            slots.append(jnp.where(m // row_span == row, near, received[s]))
        chosen.append(jnp.stack(slots))
    return chosen, partners[0]


def attend(grouped, keys, values, key_positions, positions, live_length, slot_count):
    row_count, _, group_count, group_portion, _ = grouped.shape
    inverse = 1.0 / math.sqrt(HEAD_SIZE)

    def update(running, key_block, value_block, block_positions):
        run_max, run_total, accumulated = running
        block_length = key_block.shape[0]
        heads_of_keys = key_block.reshape(block_length, group_count, HEAD_SIZE)
        heads_of_values = value_block.reshape(block_length, slot_count, group_count, HEAD_SIZE)
        scores = (
            jnp.einsum(
                "rsgjd,kgd->sgjrk", grouped, heads_of_keys, preferred_element_type=jnp.float32
            )
            * inverse
        )
        visible = (block_positions[None, :] <= positions[:, None]) & (
            block_positions[None, :] < live_length
        )
        masked = jnp.where(visible, scores, -1e30)
        new_max = jnp.maximum(run_max, jnp.max(masked, axis=-1))
        weights = jnp.where(visible, jnp.exp(masked - new_max[..., None]), 0.0)
        factor = jnp.exp(run_max - new_max)
        new_total = run_total * factor + jnp.sum(weights, axis=-1)
        new_accumulated = accumulated * factor[..., None] + jnp.einsum(
            "sgjrk,ksgd->sgjrd",
            weights.astype(jnp.bfloat16),
            heads_of_values,
            preferred_element_type=jnp.float32,
        )
        return (new_max, new_total, new_accumulated)

    initial = (
        jnp.full((slot_count, group_count, group_portion, row_count), -1e30, jnp.float32),
        jnp.zeros((slot_count, group_count, group_portion, row_count), jnp.float32),
        jnp.zeros((slot_count, group_count, group_portion, row_count, HEAD_SIZE), jnp.float32),
    )
    piece_rows = keys.shape[0]
    step_rows = block_rows(piece_rows)

    def advance(block_index, current):
        offset = block_index * step_rows
        key_block = lax.dynamic_slice_in_dim(keys, offset, step_rows, 0)
        value_block = lax.dynamic_slice_in_dim(values, offset, step_rows, 0)
        block_positions = lax.dynamic_slice_in_dim(key_positions, offset, step_rows, 0)
        return update(current, key_block, value_block, block_positions)

    run_max, run_total, accumulated = lax.fori_loop(0, piece_rows // step_rows, advance, initial)
    result = accumulated / run_total[..., None]
    return (
        jnp.transpose(result, (0, 3, 1, 2, 4))
        .reshape(slot_count, row_count, group_count * group_portion * HEAD_SIZE)
        .astype(jnp.bfloat16)
    )


def per_device(
    activations,
    query_base,
    key_base,
    plain_value_rows,
    query_down,
    query_up,
    value_down,
    value_raise_factor,
    member_lists,
    prompt_lengths,
):
    row_count = activations.shape[1]
    member_ids = member_lists[0]
    slot_count = member_ids.shape[0]
    up_width = query_up.shape[2]
    group_count = key_base.shape[2] // HEAD_SIZE
    ctx = lax.axis_index("ctx")
    positions = ctx * row_count + jnp.arange(row_count, dtype=jnp.int32)
    downs = jnp.stack([query_down, value_down], axis=1)
    ups = jnp.concatenate([query_up, value_raise_factor], axis=2)
    early = lax.axis_size("ctx") == 2 and lax.axis_size("req") == 4
    prepare = None
    carried = {}
    if early:
        def prepare(value):
            local_rows = lax.optimization_barrier((activations[0], value))[0]
            other_rows = swap(local_rows, "ctx", 1)
            carried["tokens"] = jnp.concatenate([local_rows, other_rows], axis=0)
            value = lax.optimization_barrier((value, other_rows))[0]
            return jnp.concatenate([value, swap(value, "ctx", 1)], axis=1)

    (down_half, up_half), first = select_members(
        (downs, ups), member_ids, member_lists, prepare
    )
    ups = up_half if early else ctx_gather(up_half, 1, False)
    up_query = ups[..., :up_width]
    up_value = ups[..., up_width:]
    if lax.axis_size("ctx") == 2:
        local_rows, value_rows, keys, _ = lax.optimization_barrier(
            (activations[0], plain_value_rows[0], key_base[0], first)
        )
        tokens = carried["tokens"] if "tokens" in carried else ctx_gather(local_rows, 0, False)
        partial = jnp.einsum("rd,sfkd->rfsk", tokens, down_half, preferred_element_type=jnp.float32)
        mine = mp_sum(partial).astype(jnp.bfloat16)
        theirs = swap(mine, "ctx", 1)
        theirs = jnp.concatenate([theirs[row_count:], theirs[:row_count]], axis=0)
        ranks = jnp.concatenate([mine, theirs], axis=3)
        value_rows = ctx_gather(value_rows, 0, False)
        keys = ctx_gather(keys, 0, False)
        own_keys = jnp.arange(row_count, dtype=jnp.int32)
        key_positions = jnp.concatenate(
            [ctx * row_count + own_keys, (1 - ctx) * row_count + own_keys]
        )
        rank_query = ranks[:row_count, 0]
        rank_value = ranks[:, 1]
    else:
        downs = ctx_gather(down_half, 2, False)
        partial = jnp.einsum(
            "rd,sfkd->rfsk", activations[0], downs, preferred_element_type=jnp.float32
        )
        ranks = mp_sum(partial).astype(jnp.bfloat16)
        rank_query = ranks[:, 0]
        rank_value = ranks[:, 1]
        value_rows = plain_value_rows[0]
        keys = ctx_gather(key_base[0], 0, True)
        key_positions = jnp.arange(keys.shape[0], dtype=jnp.int32)
    query_matrix = (
        query_base[0][:, None, :]
        + jnp.einsum("rsk,skc->rsc", rank_query, up_query, preferred_element_type=jnp.float32)
    ).astype(jnp.bfloat16)
    group_portion = query_matrix.shape[2] // (group_count * HEAD_SIZE)
    grouped = query_matrix.reshape(row_count, slot_count, group_count, group_portion, HEAD_SIZE)
    built = (
        value_rows[:, None, :]
        + jnp.einsum("rsk,skc->rsc", rank_value, up_value, preferred_element_type=jnp.float32)
    ).astype(jnp.bfloat16)
    values = built.reshape(built.shape[0], slot_count * group_count * HEAD_SIZE)
    if lax.axis_size("ctx") != 2:
        values = ctx_gather(values, 0, True)
    result = attend(
        grouped, keys, values, key_positions, positions, prompt_lengths[0], slot_count
    )
    return result[:, None]


def solution(mesh):
    in_specs = (
        P("req", "ctx", "mp"),
        P("req", "ctx", "mp"),
        P("req", "ctx", "mp"),
        P("req", "ctx", "mp"),
        P("req", "ctx", "mp"),
        P("req", "ctx", "mp"),
        P("req", "ctx", "mp"),
        P("req", "ctx", "mp"),
        P("req", None),
        P("req"),
    )
    out_specs = P(None, "req", "ctx", "mp")
    return jax.shard_map(
        per_device, mesh=mesh, in_specs=in_specs, out_specs=out_specs, check_vma=False
    )
```

```python
import math

import jax
import jax.numpy as jnp
from jax import lax
from jax.sharding import PartitionSpec as P

HEAD_SIZE = 128


def block_rows(total_rows):
    if total_rows <= 512:
        return total_rows
    for candidate in range(512, 0, -1):
        if total_rows % candidate == 0:
            return candidate
    return total_rows


def swap(value, axis, bit):
    size = lax.axis_size(axis)
    return lax.ppermute(value, axis, [(i, i ^ bit) for i in range(size)])


def ctx_gather(mine, dim, ordered):
    if lax.axis_size("ctx") == 2:
        other = swap(mine, "ctx", 1)
        if not ordered:
            return jnp.concatenate([mine, other], axis=dim)
        first = lax.axis_index("ctx") == 0
        low = jnp.where(first, mine, other)
        high = jnp.where(first, other, mine)
        return jnp.concatenate([low, high], axis=dim)
    return lax.all_gather(mine, "ctx", axis=dim, tiled=True)


def mp_sum(value):
    size = lax.axis_size("mp")
    if size & (size - 1):
        return lax.psum(value, "mp")
    total = value
    for bit in range(1, size):
        total = total + swap(value, "mp", bit)
    return total


def select_members(factor_set, member_ids, member_lists, prepare=None):
    local_count = factor_set[0].shape[0]
    req_size = lax.axis_size("req")
    if req_size != 4:
        everything = [lax.all_gather(f, "req", axis=0, tiled=True) for f in factor_set]
        return [
            jnp.stack([lax.dynamic_index_in_dim(f, m, 0, keepdims=False) for m in member_ids])
            for f in everything
        ], everything[0]
    req = lax.axis_index("req")
    core = req % 2
    row = req // 2
    row_span = 2 * local_count
    far_ids = swap(member_lists, "req", 2)[0]

    def pick(own, partner, index):
        mine = lax.dynamic_index_in_dim(own, index % local_count, 0, keepdims=False)
        theirs = lax.dynamic_index_in_dim(partner, index % local_count, 0, keepdims=False)
        return jnp.where(index // local_count == core, mine, theirs)

    owns = []
    partners = []
    incoming = []
    previous = None
    for own in factor_set:
        if previous is not None:
            own = lax.optimization_barrier((own, previous[0]))[0]
            if prepare is not None:
                own = prepare(own, previous)
        partner = swap(own, "req", 1)
        outgoing = jnp.stack(
            [pick(own, partner, far_ids[s] % row_span) for s in range(far_ids.shape[0])]
        )
        if previous is not None:
            outgoing = lax.optimization_barrier((outgoing, previous[1]))[0]
        received = swap(outgoing, "req", 2)
        owns.append(own)
        partners.append(partner)
        incoming.append(received)
        previous = (partner, received)
    chosen = []
    for own, partner, received in zip(owns, partners, incoming):
        slots = []
        for s in range(member_ids.shape[0]):
            m = member_ids[s]
            near = pick(own, partner, m % row_span)
            slots.append(jnp.where(m // row_span == row, near, received[s]))
        chosen.append(jnp.stack(slots))
    return chosen, partners[0]


def attend(grouped, keys, values, key_positions, positions, live_length, slot_count):
    row_count, _, group_count, group_portion, _ = grouped.shape
    inverse = 1.0 / math.sqrt(HEAD_SIZE)

    def update(running, key_block, value_block, block_positions):
        run_max, run_total, accumulated = running
        block_length = key_block.shape[0]
        heads_of_keys = key_block.reshape(block_length, group_count, HEAD_SIZE)
        heads_of_values = value_block.reshape(block_length, slot_count, group_count, HEAD_SIZE)
        scores = (
            jnp.einsum(
                "rsgjd,kgd->sgjrk", grouped, heads_of_keys, preferred_element_type=jnp.float32
            )
            * inverse
        )
        visible = (block_positions[None, :] <= positions[:, None]) & (
            block_positions[None, :] < live_length
        )
        masked = jnp.where(visible, scores, -1e30)
        new_max = jnp.maximum(run_max, jnp.max(masked, axis=-1))
        weights = jnp.where(visible, jnp.exp(masked - new_max[..., None]), 0.0)
        factor = jnp.exp(run_max - new_max)
        new_total = run_total * factor + jnp.sum(weights, axis=-1)
        new_accumulated = accumulated * factor[..., None] + jnp.einsum(
            "sgjrk,ksgd->sgjrd",
            weights.astype(jnp.bfloat16),
            heads_of_values,
            preferred_element_type=jnp.float32,
        )
        return (new_max, new_total, new_accumulated)

    initial = (
        jnp.full((slot_count, group_count, group_portion, row_count), -1e30, jnp.float32),
        jnp.zeros((slot_count, group_count, group_portion, row_count), jnp.float32),
        jnp.zeros((slot_count, group_count, group_portion, row_count, HEAD_SIZE), jnp.float32),
    )
    piece_rows = keys.shape[0]
    step_rows = block_rows(piece_rows)

    def advance(block_index, current):
        offset = block_index * step_rows
        key_block = lax.dynamic_slice_in_dim(keys, offset, step_rows, 0)
        value_block = lax.dynamic_slice_in_dim(values, offset, step_rows, 0)
        block_positions = lax.dynamic_slice_in_dim(key_positions, offset, step_rows, 0)
        return update(current, key_block, value_block, block_positions)

    run_max, run_total, accumulated = lax.fori_loop(0, piece_rows // step_rows, advance, initial)
    result = accumulated / run_total[..., None]
    return (
        jnp.transpose(result, (0, 3, 1, 2, 4))
        .reshape(slot_count, row_count, group_count * group_portion * HEAD_SIZE)
        .astype(jnp.bfloat16)
    )


def per_device(
    activations,
    query_base,
    key_base,
    plain_value_rows,
    query_down,
    query_up,
    value_down,
    value_raise_factor,
    member_lists,
    prompt_lengths,
):
    row_count = activations.shape[1]
    member_ids = member_lists[0]
    slot_count = member_ids.shape[0]
    up_width = query_up.shape[2]
    group_count = key_base.shape[2] // HEAD_SIZE
    ctx = lax.axis_index("ctx")
    positions = ctx * row_count + jnp.arange(row_count, dtype=jnp.int32)
    downs = jnp.stack([query_down, value_down], axis=1)
    ups = jnp.concatenate([query_up, value_raise_factor], axis=2)
    early = lax.axis_size("ctx") == 2 and lax.axis_size("req") == 4
    prepare = None
    carried = {}
    if early:
        def prepare(value, previous):
            local_rows = lax.optimization_barrier((activations[0], value))[0]
            other_rows = swap(local_rows, "ctx", 1)
            carried["tokens"] = jnp.concatenate([local_rows, other_rows], axis=0)
            value = lax.optimization_barrier((value, other_rows, previous[1]))[0]
            return jnp.concatenate([value, swap(value, "ctx", 1)], axis=1)

    (down_half, up_half), first = select_members(
        (downs, ups), member_ids, member_lists, prepare
    )
    ups = up_half if early else ctx_gather(up_half, 1, False)
    up_query = ups[..., :up_width]
    up_value = ups[..., up_width:]
    if lax.axis_size("ctx") == 2:
        local_rows, value_rows, keys, _ = lax.optimization_barrier(
            (activations[0], plain_value_rows[0], key_base[0], first)
        )
        tokens = carried["tokens"] if "tokens" in carried else ctx_gather(local_rows, 0, False)
        partial = jnp.einsum("rd,sfkd->rfsk", tokens, down_half, preferred_element_type=jnp.float32)
        mine = mp_sum(partial).astype(jnp.bfloat16)
        theirs = swap(mine, "ctx", 1)
        theirs = jnp.concatenate([theirs[row_count:], theirs[:row_count]], axis=0)
        ranks = jnp.concatenate([mine, theirs], axis=3)
        value_rows = ctx_gather(value_rows, 0, False)
        keys = ctx_gather(keys, 0, False)
        own_keys = jnp.arange(row_count, dtype=jnp.int32)
        key_positions = jnp.concatenate(
            [ctx * row_count + own_keys, (1 - ctx) * row_count + own_keys]
        )
        rank_query = ranks[:row_count, 0]
        rank_value = ranks[:, 1]
    else:
        downs = ctx_gather(down_half, 2, False)
        partial = jnp.einsum(
            "rd,sfkd->rfsk", activations[0], downs, preferred_element_type=jnp.float32
        )
        ranks = mp_sum(partial).astype(jnp.bfloat16)
        rank_query = ranks[:, 0]
        rank_value = ranks[:, 1]
        value_rows = plain_value_rows[0]
        keys = ctx_gather(key_base[0], 0, True)
        key_positions = jnp.arange(keys.shape[0], dtype=jnp.int32)
    query_matrix = (
        query_base[0][:, None, :]
        + jnp.einsum("rsk,skc->rsc", rank_query, up_query, preferred_element_type=jnp.float32)
    ).astype(jnp.bfloat16)
    group_portion = query_matrix.shape[2] // (group_count * HEAD_SIZE)
    grouped = query_matrix.reshape(row_count, slot_count, group_count, group_portion, HEAD_SIZE)
    built = (
        value_rows[:, None, :]
        + jnp.einsum("rsk,skc->rsc", rank_value, up_value, preferred_element_type=jnp.float32)
    ).astype(jnp.bfloat16)
    values = built.reshape(built.shape[0], slot_count * group_count * HEAD_SIZE)
    if lax.axis_size("ctx") != 2:
        values = ctx_gather(values, 0, True)
    result = attend(
        grouped, keys, values, key_positions, positions, prompt_lengths[0], slot_count
    )
    return result[:, None]


def solution(mesh):
    in_specs = (
        P("req", "ctx", "mp"),
        P("req", "ctx", "mp"),
        P("req", "ctx", "mp"),
        P("req", "ctx", "mp"),
        P("req", "ctx", "mp"),
        P("req", "ctx", "mp"),
        P("req", "ctx", "mp"),
        P("req", "ctx", "mp"),
        P("req", None),
        P("req"),
    )
    out_specs = P(None, "req", "ctx", "mp")
    return jax.shard_map(
        per_device, mesh=mesh, in_specs=in_specs, out_specs=out_specs, check_vma=False
    )
```

```python
import math

import jax
import jax.numpy as jnp
from jax import lax
from jax.sharding import PartitionSpec as P

HEAD_SIZE = 128


def block_rows(total_rows):
    if total_rows <= 512:
        return total_rows
    for candidate in range(512, 0, -1):
        if total_rows % candidate == 0:
            return candidate
    return total_rows


def swap(value, axis, bit):
    size = lax.axis_size(axis)
    return lax.ppermute(value, axis, [(i, i ^ bit) for i in range(size)])


def ctx_gather(mine, dim, ordered):
    if lax.axis_size("ctx") == 2:
        other = swap(mine, "ctx", 1)
        if not ordered:
            return jnp.concatenate([mine, other], axis=dim)
        first = lax.axis_index("ctx") == 0
        low = jnp.where(first, mine, other)
        high = jnp.where(first, other, mine)
        return jnp.concatenate([low, high], axis=dim)
    return lax.all_gather(mine, "ctx", axis=dim, tiled=True)


def mp_sum(value):
    size = lax.axis_size("mp")
    if size & (size - 1):
        return lax.psum(value, "mp")
    total = value
    for bit in range(1, size):
        total = total + swap(value, "mp", bit)
    return total


def select_members(factor_set, member_ids, member_lists, prepare=None):
    local_count = factor_set[0].shape[0]
    req_size = lax.axis_size("req")
    if req_size != 4:
        everything = [lax.all_gather(f, "req", axis=0, tiled=True) for f in factor_set]
        return [
            jnp.stack([lax.dynamic_index_in_dim(f, m, 0, keepdims=False) for m in member_ids])
            for f in everything
        ], everything[0]
    req = lax.axis_index("req")
    core = req % 2
    row = req // 2
    row_span = 2 * local_count
    far_ids = swap(member_lists, "req", 2)[0]

    def pick(own, partner, index):
        mine = lax.dynamic_index_in_dim(own, index % local_count, 0, keepdims=False)
        theirs = lax.dynamic_index_in_dim(partner, index % local_count, 0, keepdims=False)
        return jnp.where(index // local_count == core, mine, theirs)

    def choose(own, partner, received):
        slots = []
        for s in range(member_ids.shape[0]):
            m = member_ids[s]
            near = pick(own, partner, m % row_span)
            slots.append(jnp.where(m // row_span == row, near, received[s]))
        return jnp.stack(slots)

    owns = []
    partners = []
    incoming = []
    previous = None
    for own in factor_set:
        if previous is not None:
            own = lax.optimization_barrier((own, previous[0]))[0]
            if prepare is not None:
                own = prepare(own, owns[-1], previous, choose)
        partner = swap(own, "req", 1)
        outgoing = jnp.stack(
            [pick(own, partner, far_ids[s] % row_span) for s in range(far_ids.shape[0])]
        )
        if previous is not None:
            outgoing = lax.optimization_barrier((outgoing, previous[1]))[0]
        received = swap(outgoing, "req", 2)
        owns.append(own)
        partners.append(partner)
        incoming.append(received)
        previous = (partner, received)
    chosen = [choose(*parts) for parts in zip(owns, partners, incoming)]
    return chosen, partners[0]


def attend(grouped, keys, values, key_positions, positions, live_length, slot_count):
    row_count, _, group_count, group_portion, _ = grouped.shape
    inverse = 1.0 / math.sqrt(HEAD_SIZE)

    def update(running, key_block, value_block, block_positions):
        run_max, run_total, accumulated = running
        block_length = key_block.shape[0]
        heads_of_keys = key_block.reshape(block_length, group_count, HEAD_SIZE)
        heads_of_values = value_block.reshape(block_length, slot_count, group_count, HEAD_SIZE)
        scores = (
            jnp.einsum(
                "rsgjd,kgd->sgjrk", grouped, heads_of_keys, preferred_element_type=jnp.float32
            )
            * inverse
        )
        visible = (block_positions[None, :] <= positions[:, None]) & (
            block_positions[None, :] < live_length
        )
        masked = jnp.where(visible, scores, -1e30)
        new_max = jnp.maximum(run_max, jnp.max(masked, axis=-1))
        weights = jnp.where(visible, jnp.exp(masked - new_max[..., None]), 0.0)
        factor = jnp.exp(run_max - new_max)
        new_total = run_total * factor + jnp.sum(weights, axis=-1)
        new_accumulated = accumulated * factor[..., None] + jnp.einsum(
            "sgjrk,ksgd->sgjrd",
            weights.astype(jnp.bfloat16),
            heads_of_values,
            preferred_element_type=jnp.float32,
        )
        return (new_max, new_total, new_accumulated)

    initial = (
        jnp.full((slot_count, group_count, group_portion, row_count), -1e30, jnp.float32),
        jnp.zeros((slot_count, group_count, group_portion, row_count), jnp.float32),
        jnp.zeros((slot_count, group_count, group_portion, row_count, HEAD_SIZE), jnp.float32),
    )
    piece_rows = keys.shape[0]
    step_rows = block_rows(piece_rows)

    def advance(block_index, current):
        offset = block_index * step_rows
        key_block = lax.dynamic_slice_in_dim(keys, offset, step_rows, 0)
        value_block = lax.dynamic_slice_in_dim(values, offset, step_rows, 0)
        block_positions = lax.dynamic_slice_in_dim(key_positions, offset, step_rows, 0)
        return update(current, key_block, value_block, block_positions)

    run_max, run_total, accumulated = lax.fori_loop(0, piece_rows // step_rows, advance, initial)
    result = accumulated / run_total[..., None]
    return (
        jnp.transpose(result, (0, 3, 1, 2, 4))
        .reshape(slot_count, row_count, group_count * group_portion * HEAD_SIZE)
        .astype(jnp.bfloat16)
    )


def per_device(
    activations,
    query_base,
    key_base,
    plain_value_rows,
    query_down,
    query_up,
    value_down,
    value_raise_factor,
    member_lists,
    prompt_lengths,
):
    row_count = activations.shape[1]
    member_ids = member_lists[0]
    slot_count = member_ids.shape[0]
    up_width = query_up.shape[2]
    group_count = key_base.shape[2] // HEAD_SIZE
    ctx = lax.axis_index("ctx")
    positions = ctx * row_count + jnp.arange(row_count, dtype=jnp.int32)
    downs = jnp.stack([query_down, value_down], axis=1)
    ups = jnp.concatenate([query_up, value_raise_factor], axis=2)
    early = lax.axis_size("ctx") == 2 and lax.axis_size("req") == 4
    prepare = None
    carried = {}
    if early:
        def prepare(value, down_own, previous, choose):
            local_rows = lax.optimization_barrier((activations[0], value))[0]
            tokens = ctx_gather(local_rows, 0, False)
            half = choose(down_own, *previous)
            carried["partial"] = jnp.einsum(
                "rd,sfkd->rfsk", tokens, half, preferred_element_type=jnp.float32
            )
            value = lax.optimization_barrier((value, carried["partial"]))[0]
            return ctx_gather(value, 1, False)

    (down_half, up_half), first = select_members(
        (downs, ups), member_ids, member_lists, prepare
    )
    ups = up_half if early else ctx_gather(up_half, 1, False)
    up_query = ups[..., :up_width]
    up_value = ups[..., up_width:]
    if lax.axis_size("ctx") == 2:
        local_rows, value_rows, keys, _ = lax.optimization_barrier(
            (activations[0], plain_value_rows[0], key_base[0], first)
        )
        if "partial" in carried:
            partial = carried["partial"]
        else:
            tokens = ctx_gather(local_rows, 0, False)
            partial = jnp.einsum(
                "rd,sfkd->rfsk", tokens, down_half, preferred_element_type=jnp.float32
            )
        mine = mp_sum(partial).astype(jnp.bfloat16)
        theirs = swap(mine, "ctx", 1)
        theirs = jnp.concatenate([theirs[row_count:], theirs[:row_count]], axis=0)
        ranks = jnp.concatenate([mine, theirs], axis=3)
        value_rows = ctx_gather(value_rows, 0, False)
        keys = ctx_gather(keys, 0, False)
        own_keys = jnp.arange(row_count, dtype=jnp.int32)
        key_positions = jnp.concatenate(
            [ctx * row_count + own_keys, (1 - ctx) * row_count + own_keys]
        )
        rank_query = ranks[:row_count, 0]
        rank_value = ranks[:, 1]
    else:
        downs = ctx_gather(down_half, 2, False)
        partial = jnp.einsum(
            "rd,sfkd->rfsk", activations[0], downs, preferred_element_type=jnp.float32
        )
        ranks = mp_sum(partial).astype(jnp.bfloat16)
        rank_query = ranks[:, 0]
        rank_value = ranks[:, 1]
        value_rows = plain_value_rows[0]
        keys = ctx_gather(key_base[0], 0, True)
        key_positions = jnp.arange(keys.shape[0], dtype=jnp.int32)
    query_matrix = (
        query_base[0][:, None, :]
        + jnp.einsum("rsk,skc->rsc", rank_query, up_query, preferred_element_type=jnp.float32)
    ).astype(jnp.bfloat16)
    group_portion = query_matrix.shape[2] // (group_count * HEAD_SIZE)
    grouped = query_matrix.reshape(row_count, slot_count, group_count, group_portion, HEAD_SIZE)
    built = (
        value_rows[:, None, :]
        + jnp.einsum("rsk,skc->rsc", rank_value, up_value, preferred_element_type=jnp.float32)
    ).astype(jnp.bfloat16)
    values = built.reshape(built.shape[0], slot_count * group_count * HEAD_SIZE)
    if lax.axis_size("ctx") != 2:
        values = ctx_gather(values, 0, True)
    result = attend(
        grouped, keys, values, key_positions, positions, prompt_lengths[0], slot_count
    )
    return result[:, None]


def solution(mesh):
    in_specs = (
        P("req", "ctx", "mp"),
        P("req", "ctx", "mp"),
        P("req", "ctx", "mp"),
        P("req", "ctx", "mp"),
        P("req", "ctx", "mp"),
        P("req", "ctx", "mp"),
        P("req", "ctx", "mp"),
        P("req", "ctx", "mp"),
        P("req", None),
        P("req"),
    )
    out_specs = P(None, "req", "ctx", "mp")
    return jax.shard_map(
        per_device, mesh=mesh, in_specs=in_specs, out_specs=out_specs, check_vma=False
    )
```

```python
import math

import jax
import jax.numpy as jnp
from jax import lax
from jax.sharding import PartitionSpec as P

HEAD_SIZE = 128


def block_rows(total_rows):
    if total_rows <= 512:
        return total_rows
    for candidate in range(512, 0, -1):
        if total_rows % candidate == 0:
            return candidate
    return total_rows


def swap(value, axis, bit):
    size = lax.axis_size(axis)
    return lax.ppermute(value, axis, [(i, i ^ bit) for i in range(size)])


def ctx_gather(mine, dim, ordered):
    if lax.axis_size("ctx") == 2:
        other = swap(mine, "ctx", 1)
        if not ordered:
            return jnp.concatenate([mine, other], axis=dim)
        first = lax.axis_index("ctx") == 0
        low = jnp.where(first, mine, other)
        high = jnp.where(first, other, mine)
        return jnp.concatenate([low, high], axis=dim)
    return lax.all_gather(mine, "ctx", axis=dim, tiled=True)


def mp_sum(value):
    size = lax.axis_size("mp")
    if size & (size - 1):
        return lax.psum(value, "mp")
    total = value
    for bit in range(1, size):
        total = total + swap(value, "mp", bit)
    return total


def select_members(factor_set, member_ids, member_lists, prepare=None):
    local_count = factor_set[0].shape[0]
    req_size = lax.axis_size("req")
    if req_size != 4:
        everything = [lax.all_gather(f, "req", axis=0, tiled=True) for f in factor_set]
        return [
            jnp.stack([lax.dynamic_index_in_dim(f, m, 0, keepdims=False) for m in member_ids])
            for f in everything
        ], everything[0]
    req = lax.axis_index("req")
    core = req % 2
    row = req // 2
    row_span = 2 * local_count
    far_ids = swap(member_lists, "req", 2)[0]

    def pick(own, partner, index):
        mine = lax.dynamic_index_in_dim(own, index % local_count, 0, keepdims=False)
        theirs = lax.dynamic_index_in_dim(partner, index % local_count, 0, keepdims=False)
        return jnp.where(index // local_count == core, mine, theirs)

    owns = []
    partners = []
    incoming = []
    previous = None
    for own in factor_set:
        if previous is not None:
            own = lax.optimization_barrier((own, previous[0]))[0]
            if prepare is not None:
                own = prepare(own)
        partner = swap(own, "req", 1)
        outgoing = jnp.stack(
            [pick(own, partner, far_ids[s] % row_span) for s in range(far_ids.shape[0])]
        )
        if previous is not None:
            outgoing = lax.optimization_barrier((outgoing, previous[1]))[0]
        received = swap(outgoing, "req", 2)
        owns.append(own)
        partners.append(partner)
        incoming.append(received)
        previous = (partner, received)
    chosen = []
    for own, partner, received in zip(owns, partners, incoming):
        slots = []
        for s in range(member_ids.shape[0]):
            m = member_ids[s]
            near = pick(own, partner, m % row_span)
            slots.append(jnp.where(m // row_span == row, near, received[s]))
        chosen.append(jnp.stack(slots))
    return chosen, partners[0]


def attend(grouped, keys, values, key_positions, positions, live_length, slot_count):
    row_count, _, group_count, group_portion, _ = grouped.shape
    inverse = 1.0 / math.sqrt(HEAD_SIZE)

    def update(running, key_block, value_block, block_positions):
        run_max, run_total, accumulated = running
        block_length = key_block.shape[0]
        heads_of_keys = key_block.reshape(block_length, group_count, HEAD_SIZE)
        heads_of_values = value_block.reshape(block_length, slot_count, group_count, HEAD_SIZE)
        scores = (
            jnp.einsum(
                "rsgjd,kgd->sgjrk", grouped, heads_of_keys, preferred_element_type=jnp.float32
            )
            * inverse
        )
        visible = (block_positions[None, :] <= positions[:, None]) & (
            block_positions[None, :] < live_length
        )
        masked = jnp.where(visible, scores, -1e30)
        new_max = jnp.maximum(run_max, jnp.max(masked, axis=-1))
        weights = jnp.where(visible, jnp.exp(masked - new_max[..., None]), 0.0)
        factor = jnp.exp(run_max - new_max)
        new_total = run_total * factor + jnp.sum(weights, axis=-1)
        new_accumulated = accumulated * factor[..., None] + jnp.einsum(
            "sgjrk,ksgd->sgjrd",
            weights.astype(jnp.bfloat16),
            heads_of_values,
            preferred_element_type=jnp.float32,
        )
        return (new_max, new_total, new_accumulated)

    initial = (
        jnp.full((slot_count, group_count, group_portion, row_count), -1e30, jnp.float32),
        jnp.zeros((slot_count, group_count, group_portion, row_count), jnp.float32),
        jnp.zeros((slot_count, group_count, group_portion, row_count, HEAD_SIZE), jnp.float32),
    )
    piece_rows = keys.shape[0]
    step_rows = block_rows(piece_rows)

    def advance(block_index, current):
        offset = block_index * step_rows
        key_block = lax.dynamic_slice_in_dim(keys, offset, step_rows, 0)
        value_block = lax.dynamic_slice_in_dim(values, offset, step_rows, 0)
        block_positions = lax.dynamic_slice_in_dim(key_positions, offset, step_rows, 0)
        return update(current, key_block, value_block, block_positions)

    run_max, run_total, accumulated = lax.fori_loop(0, piece_rows // step_rows, advance, initial)
    result = accumulated / run_total[..., None]
    return (
        jnp.transpose(result, (0, 3, 1, 2, 4))
        .reshape(slot_count, row_count, group_count * group_portion * HEAD_SIZE)
        .astype(jnp.bfloat16)
    )


def per_device(
    activations,
    query_base,
    key_base,
    plain_value_rows,
    query_down,
    query_up,
    value_down,
    value_raise_factor,
    member_lists,
    prompt_lengths,
):
    row_count = activations.shape[1]
    member_ids = member_lists[0]
    slot_count = member_ids.shape[0]
    up_width = query_up.shape[2]
    group_count = key_base.shape[2] // HEAD_SIZE
    ctx = lax.axis_index("ctx")
    positions = ctx * row_count + jnp.arange(row_count, dtype=jnp.int32)
    downs = jnp.stack([query_down, value_down], axis=1)
    ups = jnp.concatenate([query_up, value_raise_factor], axis=2)
    early = lax.axis_size("ctx") == 2 and lax.axis_size("req") == 4
    prepare = (lambda value: ctx_gather(value, 1, False)) if early else None
    (down_half, up_half), first = select_members(
        (downs, ups), member_ids, member_lists, prepare
    )
    ups = up_half if early else ctx_gather(up_half, 1, False)
    up_query = ups[..., :up_width]
    up_value = ups[..., up_width:]
    if lax.axis_size("ctx") == 2:
        local_rows, _ = lax.optimization_barrier((activations[0], first))
        value_rows, keys = plain_value_rows[0], key_base[0]
        tokens = ctx_gather(local_rows, 0, False)
        partial = jnp.einsum("rd,sfkd->rfsk", tokens, down_half, preferred_element_type=jnp.float32)
        mine = mp_sum(partial).astype(jnp.bfloat16)
        theirs = swap(mine, "ctx", 1)
        theirs = jnp.concatenate([theirs[row_count:], theirs[:row_count]], axis=0)
        ranks = jnp.concatenate([mine, theirs], axis=3)
        value_rows = ctx_gather(value_rows, 0, False)
        keys = ctx_gather(keys, 0, False)
        own_keys = jnp.arange(row_count, dtype=jnp.int32)
        key_positions = jnp.concatenate(
            [ctx * row_count + own_keys, (1 - ctx) * row_count + own_keys]
        )
        rank_query = ranks[:row_count, 0]
        rank_value = ranks[:, 1]
    else:
        downs = ctx_gather(down_half, 2, False)
        partial = jnp.einsum(
            "rd,sfkd->rfsk", activations[0], downs, preferred_element_type=jnp.float32
        )
        ranks = mp_sum(partial).astype(jnp.bfloat16)
        rank_query = ranks[:, 0]
        rank_value = ranks[:, 1]
        value_rows = plain_value_rows[0]
        keys = ctx_gather(key_base[0], 0, True)
        key_positions = jnp.arange(keys.shape[0], dtype=jnp.int32)
    query_matrix = (
        query_base[0][:, None, :]
        + jnp.einsum("rsk,skc->rsc", rank_query, up_query, preferred_element_type=jnp.float32)
    ).astype(jnp.bfloat16)
    group_portion = query_matrix.shape[2] // (group_count * HEAD_SIZE)
    grouped = query_matrix.reshape(row_count, slot_count, group_count, group_portion, HEAD_SIZE)
    built = (
        value_rows[:, None, :]
        + jnp.einsum("rsk,skc->rsc", rank_value, up_value, preferred_element_type=jnp.float32)
    ).astype(jnp.bfloat16)
    values = built.reshape(built.shape[0], slot_count * group_count * HEAD_SIZE)
    if lax.axis_size("ctx") != 2:
        values = ctx_gather(values, 0, True)
    result = attend(
        grouped, keys, values, key_positions, positions, prompt_lengths[0], slot_count
    )
    return result[:, None]


def solution(mesh):
    in_specs = (
        P("req", "ctx", "mp"),
        P("req", "ctx", "mp"),
        P("req", "ctx", "mp"),
        P("req", "ctx", "mp"),
        P("req", "ctx", "mp"),
        P("req", "ctx", "mp"),
        P("req", "ctx", "mp"),
        P("req", "ctx", "mp"),
        P("req", None),
        P("req"),
    )
    out_specs = P(None, "req", "ctx", "mp")
    return jax.shard_map(
        per_device, mesh=mesh, in_specs=in_specs, out_specs=out_specs, check_vma=False
    )
```

```python
import math

import jax
import jax.numpy as jnp
from jax import lax
from jax.sharding import PartitionSpec as P

HEAD_SIZE = 128


def block_rows(total_rows):
    if total_rows <= 512:
        return total_rows
    for candidate in range(512, 0, -1):
        if total_rows % candidate == 0:
            return candidate
    return total_rows


def swap(value, axis, bit):
    size = lax.axis_size(axis)
    return lax.ppermute(value, axis, [(i, i ^ bit) for i in range(size)])


def ctx_gather(mine, dim, ordered):
    if lax.axis_size("ctx") == 2:
        other = swap(mine, "ctx", 1)
        if not ordered:
            return jnp.concatenate([mine, other], axis=dim)
        first = lax.axis_index("ctx") == 0
        low = jnp.where(first, mine, other)
        high = jnp.where(first, other, mine)
        return jnp.concatenate([low, high], axis=dim)
    return lax.all_gather(mine, "ctx", axis=dim, tiled=True)


def mp_sum(value):
    size = lax.axis_size("mp")
    if size & (size - 1):
        return lax.psum(value, "mp")
    total = value
    for bit in range(1, size):
        total = total + swap(value, "mp", bit)
    return total


def select_members(factor_set, member_ids, member_lists, prepare=None):
    local_count = factor_set[0].shape[0]
    req_size = lax.axis_size("req")
    if req_size != 4:
        everything = [lax.all_gather(f, "req", axis=0, tiled=True) for f in factor_set]
        return [
            jnp.stack([lax.dynamic_index_in_dim(f, m, 0, keepdims=False) for m in member_ids])
            for f in everything
        ], everything[0]
    req = lax.axis_index("req")
    core = req % 2
    row = req // 2
    row_span = 2 * local_count
    far_ids = swap(member_lists, "req", 2)[0]

    def pick(own, partner, index):
        mine = lax.dynamic_index_in_dim(own, index % local_count, 0, keepdims=False)
        theirs = lax.dynamic_index_in_dim(partner, index % local_count, 0, keepdims=False)
        return jnp.where(index // local_count == core, mine, theirs)

    owns = []
    partners = []
    incoming = []
    previous = None
    for own in factor_set:
        if previous is not None:
            own = lax.optimization_barrier((own, previous[0]))[0]
            if prepare is not None:
                own = prepare(own)
        partner = swap(own, "req", 1)
        outgoing = jnp.stack(
            [pick(own, partner, far_ids[s] % row_span) for s in range(far_ids.shape[0])]
        )
        if previous is not None:
            outgoing = lax.optimization_barrier((outgoing, previous[1]))[0]
        received = swap(outgoing, "req", 2)
        owns.append(own)
        partners.append(partner)
        incoming.append(received)
        previous = (partner, received)
    chosen = []
    for own, partner, received in zip(owns, partners, incoming):
        slots = []
        for s in range(member_ids.shape[0]):
            m = member_ids[s]
            near = pick(own, partner, m % row_span)
            slots.append(jnp.where(m // row_span == row, near, received[s]))
        chosen.append(jnp.stack(slots))
    return chosen, partners[0]


def attend(grouped, keys, values, key_positions, positions, live_length, slot_count):
    row_count, _, group_count, group_portion, _ = grouped.shape
    inverse = 1.0 / math.sqrt(HEAD_SIZE)

    def update(running, key_block, value_block, block_positions):
        run_max, run_total, accumulated = running
        block_length = key_block.shape[0]
        heads_of_keys = key_block.reshape(block_length, group_count, HEAD_SIZE)
        heads_of_values = value_block.reshape(block_length, slot_count, group_count, HEAD_SIZE)
        scores = (
            jnp.einsum(
                "rsgjd,kgd->sgjrk", grouped, heads_of_keys, preferred_element_type=jnp.float32
            )
            * inverse
        )
        visible = (block_positions[None, :] <= positions[:, None]) & (
            block_positions[None, :] < live_length
        )
        masked = jnp.where(visible, scores, -1e30)
        new_max = jnp.maximum(run_max, jnp.max(masked, axis=-1))
        weights = jnp.where(visible, jnp.exp(masked - new_max[..., None]), 0.0)
        factor = jnp.exp(run_max - new_max)
        new_total = run_total * factor + jnp.sum(weights, axis=-1)
        new_accumulated = accumulated * factor[..., None] + jnp.einsum(
            "sgjrk,ksgd->sgjrd",
            weights.astype(jnp.bfloat16),
            heads_of_values,
            preferred_element_type=jnp.float32,
        )
        return (new_max, new_total, new_accumulated)

    initial = (
        jnp.full((slot_count, group_count, group_portion, row_count), -1e30, jnp.float32),
        jnp.zeros((slot_count, group_count, group_portion, row_count), jnp.float32),
        jnp.zeros((slot_count, group_count, group_portion, row_count, HEAD_SIZE), jnp.float32),
    )
    piece_rows = keys.shape[0]
    step_rows = block_rows(piece_rows)

    def advance(block_index, current):
        offset = block_index * step_rows
        key_block = lax.dynamic_slice_in_dim(keys, offset, step_rows, 0)
        value_block = lax.dynamic_slice_in_dim(values, offset, step_rows, 0)
        block_positions = lax.dynamic_slice_in_dim(key_positions, offset, step_rows, 0)
        return update(current, key_block, value_block, block_positions)

    run_max, run_total, accumulated = lax.fori_loop(0, piece_rows // step_rows, advance, initial)
    result = accumulated / run_total[..., None]
    return (
        jnp.transpose(result, (0, 3, 1, 2, 4))
        .reshape(slot_count, row_count, group_count * group_portion * HEAD_SIZE)
        .astype(jnp.bfloat16)
    )


def per_device(
    activations,
    query_base,
    key_base,
    plain_value_rows,
    query_down,
    query_up,
    value_down,
    value_raise_factor,
    member_lists,
    prompt_lengths,
):
    row_count = activations.shape[1]
    member_ids = member_lists[0]
    slot_count = member_ids.shape[0]
    up_width = query_up.shape[2]
    group_count = key_base.shape[2] // HEAD_SIZE
    ctx = lax.axis_index("ctx")
    positions = ctx * row_count + jnp.arange(row_count, dtype=jnp.int32)
    downs = jnp.stack([query_down, value_down], axis=1)
    ups = jnp.concatenate([query_up, value_raise_factor], axis=2)
    early = lax.axis_size("ctx") == 2 and lax.axis_size("req") == 4
    prepare = (lambda value: ctx_gather(value, 1, False)) if early else None
    (down_half, up_half), first = select_members(
        (downs, ups), member_ids, member_lists, prepare
    )
    ups = up_half if early else ctx_gather(up_half, 1, False)
    up_query = ups[..., :up_width]
    up_value = ups[..., up_width:]
    if lax.axis_size("ctx") == 2:
        local_rows, value_rows, keys, _ = lax.optimization_barrier(
            (activations[0], plain_value_rows[0], key_base[0], first)
        )
        tokens = ctx_gather(local_rows, 0, False)
        partial = jnp.einsum("rd,sfkd->rfsk", tokens, down_half, preferred_element_type=jnp.float32)
        mine = mp_sum(partial).astype(jnp.bfloat16)
        theirs = swap(mine, "ctx", 1)
        theirs = jnp.concatenate([theirs[row_count:], theirs[:row_count]], axis=0)
        value_rows = ctx_gather(value_rows, 0, False)
        keys = ctx_gather(keys, 0, False)
        own_keys = jnp.arange(row_count, dtype=jnp.int32)
        key_positions = jnp.concatenate(
            [ctx * row_count + own_keys, (1 - ctx) * row_count + own_keys]
        )
        half = mine.shape[3]

        query_sum = (
            jnp.einsum("rsk,skc->rsc", mine[:row_count, 0], up_query[:, :half],
                       preferred_element_type=jnp.float32)
            + jnp.einsum("rsk,skc->rsc", theirs[:row_count, 0], up_query[:, half:],
                         preferred_element_type=jnp.float32)
        )
        value_sum = (
            jnp.einsum("rsk,skc->rsc", mine[:, 1], up_value[:, :half],
                       preferred_element_type=jnp.float32)
            + jnp.einsum("rsk,skc->rsc", theirs[:, 1], up_value[:, half:],
                         preferred_element_type=jnp.float32)
        )
    else:
        downs = ctx_gather(down_half, 2, False)
        partial = jnp.einsum(
            "rd,sfkd->rfsk", activations[0], downs, preferred_element_type=jnp.float32
        )
        ranks = mp_sum(partial).astype(jnp.bfloat16)
        query_sum = jnp.einsum(
            "rsk,skc->rsc", ranks[:, 0], up_query, preferred_element_type=jnp.float32
        )
        value_sum = jnp.einsum(
            "rsk,skc->rsc", ranks[:, 1], up_value, preferred_element_type=jnp.float32
        )
        value_rows = plain_value_rows[0]
        keys = ctx_gather(key_base[0], 0, True)
        key_positions = jnp.arange(keys.shape[0], dtype=jnp.int32)
    query_matrix = (query_base[0][:, None, :] + query_sum).astype(jnp.bfloat16)
    group_portion = query_matrix.shape[2] // (group_count * HEAD_SIZE)
    grouped = query_matrix.reshape(row_count, slot_count, group_count, group_portion, HEAD_SIZE)
    built = (value_rows[:, None, :] + value_sum).astype(jnp.bfloat16)
    values = built.reshape(built.shape[0], slot_count * group_count * HEAD_SIZE)
    if lax.axis_size("ctx") != 2:
        values = ctx_gather(values, 0, True)
    result = attend(
        grouped, keys, values, key_positions, positions, prompt_lengths[0], slot_count
    )
    return result[:, None]


def solution(mesh):
    in_specs = (
        P("req", "ctx", "mp"),
        P("req", "ctx", "mp"),
        P("req", "ctx", "mp"),
        P("req", "ctx", "mp"),
        P("req", "ctx", "mp"),
        P("req", "ctx", "mp"),
        P("req", "ctx", "mp"),
        P("req", "ctx", "mp"),
        P("req", None),
        P("req"),
    )
    out_specs = P(None, "req", "ctx", "mp")
    return jax.shard_map(
        per_device, mesh=mesh, in_specs=in_specs, out_specs=out_specs, check_vma=False
    )
```

```python
import math

import jax
import jax.numpy as jnp
from jax import lax
from jax.sharding import PartitionSpec as P

HEAD_SIZE = 128


def block_rows(total_rows):
    if total_rows <= 512:
        return total_rows
    for candidate in range(512, 0, -1):
        if total_rows % candidate == 0:
            return candidate
    return total_rows


def swap(value, axis, bit):
    size = lax.axis_size(axis)
    return lax.ppermute(value, axis, [(i, i ^ bit) for i in range(size)])


def ctx_gather(mine, dim, ordered):
    if lax.axis_size("ctx") == 2:
        other = swap(mine, "ctx", 1)
        if not ordered:
            return jnp.concatenate([mine, other], axis=dim)
        first = lax.axis_index("ctx") == 0
        low = jnp.where(first, mine, other)
        high = jnp.where(first, other, mine)
        return jnp.concatenate([low, high], axis=dim)
    return lax.all_gather(mine, "ctx", axis=dim, tiled=True)


def mp_sum(value):
    size = lax.axis_size("mp")
    if size & (size - 1):
        return lax.psum(value, "mp")
    total = value
    for bit in range(1, size):
        total = total + swap(value, "mp", bit)
    return total


def select_members(factor_set, member_ids, member_lists, prepare=None):
    local_count = factor_set[0].shape[0]
    req_size = lax.axis_size("req")
    if req_size != 4:
        everything = [lax.all_gather(f, "req", axis=0, tiled=True) for f in factor_set]
        return [
            jnp.stack([lax.dynamic_index_in_dim(f, m, 0, keepdims=False) for m in member_ids])
            for f in everything
        ], everything[0]
    req = lax.axis_index("req")
    core = req % 2
    row = req // 2
    row_span = 2 * local_count
    far_ids = swap(lax.optimization_barrier((member_lists, factor_set[0]))[0], "req", 2)[0]

    def pick(own, partner, index):
        mine = lax.dynamic_index_in_dim(own, index % local_count, 0, keepdims=False)
        theirs = lax.dynamic_index_in_dim(partner, index % local_count, 0, keepdims=False)
        return jnp.where(index // local_count == core, mine, theirs)

    owns = []
    partners = []
    incoming = []
    previous = None
    for own in factor_set:
        if previous is not None:
            own = lax.optimization_barrier((own, previous[0]))[0]
            if prepare is not None:
                own = prepare(own)
        partner = swap(own, "req", 1)
        outgoing = jnp.stack(
            [pick(own, partner, far_ids[s] % row_span) for s in range(far_ids.shape[0])]
        )
        if previous is not None:
            outgoing = lax.optimization_barrier((outgoing, previous[1]))[0]
        received = swap(outgoing, "req", 2)
        owns.append(own)
        partners.append(partner)
        incoming.append(received)
        previous = (partner, received)
    chosen = []
    for own, partner, received in zip(owns, partners, incoming):
        slots = []
        for s in range(member_ids.shape[0]):
            m = member_ids[s]
            near = pick(own, partner, m % row_span)
            slots.append(jnp.where(m // row_span == row, near, received[s]))
        chosen.append(jnp.stack(slots))
    return chosen, partners[0]


def attend(grouped, keys, values, key_positions, positions, live_length, slot_count):
    row_count, _, group_count, group_portion, _ = grouped.shape
    inverse = 1.0 / math.sqrt(HEAD_SIZE)

    def update(running, key_block, value_block, block_positions):
        run_max, run_total, accumulated = running
        block_length = key_block.shape[0]
        heads_of_keys = key_block.reshape(block_length, group_count, HEAD_SIZE)
        heads_of_values = value_block.reshape(block_length, slot_count, group_count, HEAD_SIZE)
        scores = (
            jnp.einsum(
                "rsgjd,kgd->sgjrk", grouped, heads_of_keys, preferred_element_type=jnp.float32
            )
            * inverse
        )
        visible = (block_positions[None, :] <= positions[:, None]) & (
            block_positions[None, :] < live_length
        )
        masked = jnp.where(visible, scores, -1e30)
        new_max = jnp.maximum(run_max, jnp.max(masked, axis=-1))
        weights = jnp.where(visible, jnp.exp(masked - new_max[..., None]), 0.0)
        factor = jnp.exp(run_max - new_max)
        new_total = run_total * factor + jnp.sum(weights, axis=-1)
        new_accumulated = accumulated * factor[..., None] + jnp.einsum(
            "sgjrk,ksgd->sgjrd",
            weights.astype(jnp.bfloat16),
            heads_of_values,
            preferred_element_type=jnp.float32,
        )
        return (new_max, new_total, new_accumulated)

    initial = (
        jnp.full((slot_count, group_count, group_portion, row_count), -1e30, jnp.float32),
        jnp.zeros((slot_count, group_count, group_portion, row_count), jnp.float32),
        jnp.zeros((slot_count, group_count, group_portion, row_count, HEAD_SIZE), jnp.float32),
    )
    piece_rows = keys.shape[0]
    step_rows = block_rows(piece_rows)

    def advance(block_index, current):
        offset = block_index * step_rows
        key_block = lax.dynamic_slice_in_dim(keys, offset, step_rows, 0)
        value_block = lax.dynamic_slice_in_dim(values, offset, step_rows, 0)
        block_positions = lax.dynamic_slice_in_dim(key_positions, offset, step_rows, 0)
        return update(current, key_block, value_block, block_positions)

    run_max, run_total, accumulated = lax.fori_loop(0, piece_rows // step_rows, advance, initial)
    result = accumulated / run_total[..., None]
    return (
        jnp.transpose(result, (0, 3, 1, 2, 4))
        .reshape(slot_count, row_count, group_count * group_portion * HEAD_SIZE)
        .astype(jnp.bfloat16)
    )


def per_device(
    activations,
    query_base,
    key_base,
    plain_value_rows,
    query_down,
    query_up,
    value_down,
    value_raise_factor,
    member_lists,
    prompt_lengths,
):
    row_count = activations.shape[1]
    member_ids = member_lists[0]
    slot_count = member_ids.shape[0]
    up_width = query_up.shape[2]
    group_count = key_base.shape[2] // HEAD_SIZE
    ctx = lax.axis_index("ctx")
    positions = ctx * row_count + jnp.arange(row_count, dtype=jnp.int32)
    downs = jnp.stack([query_down, value_down], axis=1)
    ups = jnp.concatenate([query_up, value_raise_factor], axis=2)
    early = lax.axis_size("ctx") == 2 and lax.axis_size("req") == 4
    prepare = (lambda value: ctx_gather(value, 1, False)) if early else None
    (down_half, up_half), first = select_members(
        (downs, ups), member_ids, member_lists, prepare
    )
    ups = up_half if early else ctx_gather(up_half, 1, False)
    up_query = ups[..., :up_width]
    up_value = ups[..., up_width:]
    if lax.axis_size("ctx") == 2:
        local_rows, value_rows, keys, _ = lax.optimization_barrier(
            (activations[0], plain_value_rows[0], key_base[0], first)
        )
        tokens = ctx_gather(local_rows, 0, False)
        partial = jnp.einsum("rd,sfkd->rfsk", tokens, down_half, preferred_element_type=jnp.float32)
        mine = mp_sum(partial).astype(jnp.bfloat16)
        theirs = swap(mine, "ctx", 1)
        theirs = jnp.concatenate([theirs[row_count:], theirs[:row_count]], axis=0)
        ranks = jnp.concatenate([mine, theirs], axis=3)
        value_rows = ctx_gather(value_rows, 0, False)
        keys = ctx_gather(keys, 0, False)
        own_keys = jnp.arange(row_count, dtype=jnp.int32)
        key_positions = jnp.concatenate(
            [ctx * row_count + own_keys, (1 - ctx) * row_count + own_keys]
        )
        rank_query = ranks[:row_count, 0]
        rank_value = ranks[:, 1]
    else:
        downs = ctx_gather(down_half, 2, False)
        partial = jnp.einsum(
            "rd,sfkd->rfsk", activations[0], downs, preferred_element_type=jnp.float32
        )
        ranks = mp_sum(partial).astype(jnp.bfloat16)
        rank_query = ranks[:, 0]
        rank_value = ranks[:, 1]
        value_rows = plain_value_rows[0]
        keys = ctx_gather(key_base[0], 0, True)
        key_positions = jnp.arange(keys.shape[0], dtype=jnp.int32)
    query_matrix = (
        query_base[0][:, None, :]
        + jnp.einsum("rsk,skc->rsc", rank_query, up_query, preferred_element_type=jnp.float32)
    ).astype(jnp.bfloat16)
    group_portion = query_matrix.shape[2] // (group_count * HEAD_SIZE)
    grouped = query_matrix.reshape(row_count, slot_count, group_count, group_portion, HEAD_SIZE)
    built = (
        value_rows[:, None, :]
        + jnp.einsum("rsk,skc->rsc", rank_value, up_value, preferred_element_type=jnp.float32)
    ).astype(jnp.bfloat16)
    values = built.reshape(built.shape[0], slot_count * group_count * HEAD_SIZE)
    if lax.axis_size("ctx") != 2:
        values = ctx_gather(values, 0, True)
    result = attend(
        grouped, keys, values, key_positions, positions, prompt_lengths[0], slot_count
    )
    return result[:, None]


def solution(mesh):
    in_specs = (
        P("req", "ctx", "mp"),
        P("req", "ctx", "mp"),
        P("req", "ctx", "mp"),
        P("req", "ctx", "mp"),
        P("req", "ctx", "mp"),
        P("req", "ctx", "mp"),
        P("req", "ctx", "mp"),
        P("req", "ctx", "mp"),
        P("req", None),
        P("req"),
    )
    out_specs = P(None, "req", "ctx", "mp")
    return jax.shard_map(
        per_device, mesh=mesh, in_specs=in_specs, out_specs=out_specs, check_vma=False
    )
```

```python
import math

import jax
import jax.numpy as jnp
from jax import lax
from jax.sharding import PartitionSpec as P

HEAD_SIZE = 128


def block_rows(total_rows):
    if total_rows <= 512:
        return total_rows
    for candidate in range(512, 0, -1):
        if total_rows % candidate == 0:
            return candidate
    return total_rows


def swap(value, axis, bit):
    size = lax.axis_size(axis)
    return lax.ppermute(value, axis, [(i, i ^ bit) for i in range(size)])


def ctx_gather(mine, dim, ordered):
    if lax.axis_size("ctx") == 2:
        other = swap(mine, "ctx", 1)
        if not ordered:
            return jnp.concatenate([mine, other], axis=dim)
        first = lax.axis_index("ctx") == 0
        low = jnp.where(first, mine, other)
        high = jnp.where(first, other, mine)
        return jnp.concatenate([low, high], axis=dim)
    return lax.all_gather(mine, "ctx", axis=dim, tiled=True)


def mp_sum(value):
    size = lax.axis_size("mp")
    if size & (size - 1):
        return lax.psum(value, "mp")
    total = value
    for bit in range(1, size):
        total = total + swap(value, "mp", bit)
    return total


def select_members(factor_set, member_ids, member_lists, prepare=None):
    local_count = factor_set[0].shape[0]
    req_size = lax.axis_size("req")
    if req_size != 4:
        everything = [lax.all_gather(f, "req", axis=0, tiled=True) for f in factor_set]
        return [
            jnp.stack([lax.dynamic_index_in_dim(f, m, 0, keepdims=False) for m in member_ids])
            for f in everything
        ], everything[0]
    req = lax.axis_index("req")
    core = req % 2
    row = req // 2
    row_span = 2 * local_count
    far_ids = swap(lax.optimization_barrier((member_lists, factor_set[0]))[0], "req", 2)[0]

    def pick(own, partner, index):
        mine = lax.dynamic_index_in_dim(own, index % local_count, 0, keepdims=False)
        theirs = lax.dynamic_index_in_dim(partner, index % local_count, 0, keepdims=False)
        return jnp.where(index // local_count == core, mine, theirs)

    sent = []
    owns = []
    partners = []
    incoming = []
    previous = None
    for own in factor_set:
        if previous is not None:
            own = lax.optimization_barrier((own, previous[0], sent[-1]))[0]
            if prepare is not None:
                own = prepare(own)
        partner = swap(own, "req", 1)
        outgoing = jnp.stack(
            [pick(own, partner, far_ids[s] % row_span) for s in range(far_ids.shape[0])]
        )
        if previous is not None:
            outgoing = lax.optimization_barrier((outgoing, previous[1]))[0]
        received = swap(outgoing, "req", 2)
        sent.append(outgoing)
        owns.append(own)
        partners.append(partner)
        incoming.append(received)
        previous = (partner, received)
    chosen = []
    for own, partner, received in zip(owns, partners, incoming):
        slots = []
        for s in range(member_ids.shape[0]):
            m = member_ids[s]
            near = pick(own, partner, m % row_span)
            slots.append(jnp.where(m // row_span == row, near, received[s]))
        chosen.append(jnp.stack(slots))
    return chosen, partners[0]


def attend(grouped, keys, values, key_positions, positions, live_length, slot_count):
    row_count, _, group_count, group_portion, _ = grouped.shape
    inverse = 1.0 / math.sqrt(HEAD_SIZE)

    def update(running, key_block, value_block, block_positions):
        run_max, run_total, accumulated = running
        block_length = key_block.shape[0]
        heads_of_keys = key_block.reshape(block_length, group_count, HEAD_SIZE)
        heads_of_values = value_block.reshape(block_length, slot_count, group_count, HEAD_SIZE)
        scores = (
            jnp.einsum(
                "rsgjd,kgd->sgjrk", grouped, heads_of_keys, preferred_element_type=jnp.float32
            )
            * inverse
        )
        visible = (block_positions[None, :] <= positions[:, None]) & (
            block_positions[None, :] < live_length
        )
        masked = jnp.where(visible, scores, -1e30)
        new_max = jnp.maximum(run_max, jnp.max(masked, axis=-1))
        weights = jnp.where(visible, jnp.exp(masked - new_max[..., None]), 0.0)
        factor = jnp.exp(run_max - new_max)
        new_total = run_total * factor + jnp.sum(weights, axis=-1)
        new_accumulated = accumulated * factor[..., None] + jnp.einsum(
            "sgjrk,ksgd->sgjrd",
            weights.astype(jnp.bfloat16),
            heads_of_values,
            preferred_element_type=jnp.float32,
        )
        return (new_max, new_total, new_accumulated)

    initial = (
        jnp.full((slot_count, group_count, group_portion, row_count), -1e30, jnp.float32),
        jnp.zeros((slot_count, group_count, group_portion, row_count), jnp.float32),
        jnp.zeros((slot_count, group_count, group_portion, row_count, HEAD_SIZE), jnp.float32),
    )
    piece_rows = keys.shape[0]
    step_rows = block_rows(piece_rows)

    def advance(block_index, current):
        offset = block_index * step_rows
        key_block = lax.dynamic_slice_in_dim(keys, offset, step_rows, 0)
        value_block = lax.dynamic_slice_in_dim(values, offset, step_rows, 0)
        block_positions = lax.dynamic_slice_in_dim(key_positions, offset, step_rows, 0)
        return update(current, key_block, value_block, block_positions)

    run_max, run_total, accumulated = lax.fori_loop(0, piece_rows // step_rows, advance, initial)
    result = accumulated / run_total[..., None]
    return (
        jnp.transpose(result, (0, 3, 1, 2, 4))
        .reshape(slot_count, row_count, group_count * group_portion * HEAD_SIZE)
        .astype(jnp.bfloat16)
    )


def per_device(
    activations,
    query_base,
    key_base,
    plain_value_rows,
    query_down,
    query_up,
    value_down,
    value_raise_factor,
    member_lists,
    prompt_lengths,
):
    row_count = activations.shape[1]
    member_ids = member_lists[0]
    slot_count = member_ids.shape[0]
    up_width = query_up.shape[2]
    group_count = key_base.shape[2] // HEAD_SIZE
    ctx = lax.axis_index("ctx")
    positions = ctx * row_count + jnp.arange(row_count, dtype=jnp.int32)
    downs = jnp.stack([query_down, value_down], axis=1)
    ups = jnp.concatenate([query_up, value_raise_factor], axis=2)
    early = lax.axis_size("ctx") == 2 and lax.axis_size("req") == 4
    prepare = (lambda value: ctx_gather(value, 1, False)) if early else None
    (down_half, up_half), first = select_members(
        (downs, ups), member_ids, member_lists, prepare
    )
    ups = up_half if early else ctx_gather(up_half, 1, False)
    up_query = ups[..., :up_width]
    up_value = ups[..., up_width:]
    if lax.axis_size("ctx") == 2:
        local_rows, value_rows, keys, _ = lax.optimization_barrier(
            (activations[0], plain_value_rows[0], key_base[0], first)
        )
        tokens = ctx_gather(local_rows, 0, False)
        partial = jnp.einsum("rd,sfkd->rfsk", tokens, down_half, preferred_element_type=jnp.float32)
        mine = mp_sum(partial).astype(jnp.bfloat16)
        theirs = swap(mine, "ctx", 1)
        theirs = jnp.concatenate([theirs[row_count:], theirs[:row_count]], axis=0)
        ranks = jnp.concatenate([mine, theirs], axis=3)
        value_rows = ctx_gather(value_rows, 0, False)
        keys = ctx_gather(keys, 0, False)
        own_keys = jnp.arange(row_count, dtype=jnp.int32)
        key_positions = jnp.concatenate(
            [ctx * row_count + own_keys, (1 - ctx) * row_count + own_keys]
        )
        rank_query = ranks[:row_count, 0]
        rank_value = ranks[:, 1]
    else:
        downs = ctx_gather(down_half, 2, False)
        partial = jnp.einsum(
            "rd,sfkd->rfsk", activations[0], downs, preferred_element_type=jnp.float32
        )
        ranks = mp_sum(partial).astype(jnp.bfloat16)
        rank_query = ranks[:, 0]
        rank_value = ranks[:, 1]
        value_rows = plain_value_rows[0]
        keys = ctx_gather(key_base[0], 0, True)
        key_positions = jnp.arange(keys.shape[0], dtype=jnp.int32)
    query_matrix = (
        query_base[0][:, None, :]
        + jnp.einsum("rsk,skc->rsc", rank_query, up_query, preferred_element_type=jnp.float32)
    ).astype(jnp.bfloat16)
    group_portion = query_matrix.shape[2] // (group_count * HEAD_SIZE)
    grouped = query_matrix.reshape(row_count, slot_count, group_count, group_portion, HEAD_SIZE)
    built = (
        value_rows[:, None, :]
        + jnp.einsum("rsk,skc->rsc", rank_value, up_value, preferred_element_type=jnp.float32)
    ).astype(jnp.bfloat16)
    values = built.reshape(built.shape[0], slot_count * group_count * HEAD_SIZE)
    if lax.axis_size("ctx") != 2:
        values = ctx_gather(values, 0, True)
    result = attend(
        grouped, keys, values, key_positions, positions, prompt_lengths[0], slot_count
    )
    return result[:, None]


def solution(mesh):
    in_specs = (
        P("req", "ctx", "mp"),
        P("req", "ctx", "mp"),
        P("req", "ctx", "mp"),
        P("req", "ctx", "mp"),
        P("req", "ctx", "mp"),
        P("req", "ctx", "mp"),
        P("req", "ctx", "mp"),
        P("req", "ctx", "mp"),
        P("req", None),
        P("req"),
    )
    out_specs = P(None, "req", "ctx", "mp")
    return jax.shard_map(
        per_device, mesh=mesh, in_specs=in_specs, out_specs=out_specs, check_vma=False
    )
```
